256 devices in a mesh: space: 8 (over x_hi, y), species: 32 (over z, x_lo, core).
Axes of the slice: x: 4 (x_hi: 2, x_lo: 2; x = x_hi * 2 + x_lo), y: 4, z: 8, core: 2. Of those that a mesh axis runs over, the one named last changes fastest.
Arguments:
- dust_state: float32 [3, 128, 256, 1024], P(None, 'species', 'space'), may hold values from -4 to 4, as said below
- gas_state: float32 [3, 256, 1024], P(None, 'space'), may hold values from -2 to 2, as said below
- species_bin: int32 [128], P('species'), may hold values from 0 to 127, each once
Outputs:
- dust_out: float32 [3, 128, 256, 1024], P(None, 'species', 'space')
- gas_out: float32 [3, 256, 1024], P(None, 'space')
The draws below stay inside these ranges and needn't reach their ends.
Inputs may be any that keep to these rules, and one draw needn't show every extreme that they name: `dust_state`: component 0 (densities) lies in 0.5 to 2; the velocities lie within -4 to 4. `gas_state`: component 0 (density) lies in 0.5 to 2; the velocities lie within -2 to 2.
All inputs are finite; a program needn't handle non-finite values.
Results may differ from the reference program's by a relative error of at most 0.0003.
Values sent between devices are 32-bit elements; how exact they have to be, the bound alone decides.
No kernel may reach another device: no remote copies, remote signals or barrier semaphores. Data moves between devices by JAX's collectives and lax.ppermute only.
A program may use at most 64 MiB of HBM per device.

```python
import math
import jax
import jax.numpy as jnp
from jax import lax

NR = 1024
STEPS = 2
NSP = 128
NA = 256


def draw_dust_state(key, part):
    key_density, key_motion = jax.random.split(jax.random.fold_in(key, 11))
    density = jnp.exp(jax.random.uniform(key_density, (1, NSP, NA, NR), jnp.float32, math.log(0.5), math.log(2.0)))
    motion = jax.random.truncated_normal(key_motion, -4.0, 4.0, (2, NSP, NA, NR), jnp.float32)
    return jnp.concatenate([density, motion], axis=0)


def draw_gas_state(key, part):
    key_density, key_motion = jax.random.split(jax.random.fold_in(key, 23))
    density = jnp.exp(jax.random.uniform(key_density, (1, NA, NR), jnp.float32, math.log(0.5), math.log(2.0)))
    motion = 0.5 * jax.random.truncated_normal(key_motion, -4.0, 4.0, (2, NA, NR), jnp.float32)
    return jnp.concatenate([density, motion], axis=0)


def setup_inputs(seed: int = 0) -> dict:
    streams_of = jax.random.split(jax.random.key(seed), 4)
    return {
        "dust_state": draw_dust_state(jax.random.fold_in(streams_of[3], 71), 0),
        "gas_state": draw_gas_state(jax.random.fold_in(streams_of[3], 71), 0),
        "species_bin": jax.random.permutation(streams_of[2], NSP).astype(jnp.int32),
    }


courant = 0.25
sound_speed = 1.0
sound_sq = 1.0
stop_floor = 0.003
stop_span = 6.907755


def window(values, start, length, along):
    return lax.slice_in_dim(values, start, start + length, axis=along)


def face_divergence(density, velocity, along):
    faces = density.shape[along] - 3
    back_two = window(density, 0, faces, along)
    here = window(density, 1, faces, along)
    ahead = window(density, 2, faces, along)
    ahead_two = window(density, 3, faces, along)
    face_speed = 0.5 * (window(velocity, 1, faces, along) + window(velocity, 2, faces, along))
    flux = jnp.maximum(face_speed, 0.0) * (1.5 * here - 0.5 * back_two) + jnp.minimum(face_speed, 0.0) * (1.5 * ahead - 0.5 * ahead_two)
    return window(flux, 1, faces - 1, along) - window(flux, 0, faces - 1, along)


def moved(fluid, step_time):
    density = fluid[0]
    radial = fluid[1]
    azimuth = fluid[2]
    div_azimuth = face_divergence(density, azimuth, 1)
    inner_density = density[:, 2:-2]
    inner_radial = radial[:, 2:-2]
    zero_pad = ((0, 0), (0, 0), (2, 2))
    div_radial = face_divergence(jnp.pad(inner_density, zero_pad), jnp.pad(inner_radial, zero_pad), 2)
    new_density = inner_density - step_time * (div_azimuth + div_radial)
    gas_density = density[-1]
    inner_gas = gas_density[2:-2]
    grad_azimuth = 0.5 * (gas_density[3:-1] - gas_density[1:-3])
    edge_gas = jnp.pad(inner_gas, ((0, 0), (1, 1)), mode="edge")
    grad_radial = 0.5 * (edge_gas[:, 2:] - edge_gas[:, :-2])
    push = step_time * sound_sq / inner_gas
    gas_velocity = jnp.stack([inner_radial[-1] - push * grad_radial, azimuth[-1, 2:-2] - push * grad_azimuth])
    dust_velocity = jnp.stack([inner_radial[:-1], azimuth[:-1, 2:-2]])
    return new_density, gas_velocity, dust_velocity


def drag_terms(new_density, dust_velocity, stop_times, step_time, total_species):
    gas_new = new_density[-1]
    rate = step_time * gas_new[None] / stop_times[:, None, None]
    weight = new_density[:-1] / (total_species * gas_new[None]) * rate / (1.0 + rate)
    terms = jnp.stack([jnp.sum(weight, 0), jnp.sum(weight * dust_velocity[0], 0), jnp.sum(weight * dust_velocity[1], 0)])
    return rate, terms


def coupled_gas(gas_velocity, totals):
    return (gas_velocity + totals[1:]) / (1.0 + totals[0])


def assemble(new_density, dust_velocity, gas_next, rate):
    dust_next = (dust_velocity + rate[None] * gas_next[:, None]) / (1.0 + rate[None])
    radial = jnp.concatenate([dust_next[0], gas_next[0][None]], axis=0)
    azimuth = jnp.concatenate([dust_next[1], gas_next[1][None]], axis=0)
    return jnp.stack([new_density, radial, azimuth])


def reference(dust_state, gas_state, species_bin):
    fluid = jnp.concatenate([dust_state, gas_state[:, None]], axis=1)
    stop_times = stop_floor * jnp.exp(stop_span * species_bin.astype(jnp.float32) / (NSP - 1))
    for iteration in range(STEPS):
        speeds = jnp.abs(fluid[1]) + jnp.abs(fluid[2])
        step_time = courant / (sound_speed + jnp.max(speeds))
        wide = jnp.pad(fluid, ((0, 0), (0, 0), (2, 2), (0, 0)), mode="wrap")
        new_density, gas_velocity, dust_velocity = moved(wide, step_time)
        rate, terms = drag_terms(new_density, dust_velocity, stop_times, step_time, NSP)
        gas_next = coupled_gas(gas_velocity, terms)
        fluid = assemble(new_density, dust_velocity, gas_next, rate)
    return fluid[:, :NSP], fluid[:, NSP]
```

```python
import jax
import jax.numpy as jnp
from jax import lax
from jax.sharding import PartitionSpec as P

STEPS = 2


courant = 0.25
sound_speed = 1.0
sound_sq = 1.0
stop_floor = 0.003
stop_span = 6.907755


def padded(block, sides, width):
    for axis, dim in sides:
        count = lax.axis_size(axis)
        forward = [(i, i + 1) for i in range(count - 1)]
        forward.append((count - 1, 0))
        backward = [(target, source) for source, target in forward]
        low = lax.ppermute(
            lax.slice_in_dim(block, block.shape[dim] - width, None, axis=dim), axis, forward
        )
        high = lax.ppermute(lax.slice_in_dim(block, 0, width, axis=dim), axis, backward)
        block = jnp.concatenate([low, block, high], axis=dim)
    return block


def window(values, start, length, along):
    return lax.slice_in_dim(values, start, start + length, axis=along)


def face_divergence(density, velocity, along):
    faces = density.shape[along] - 3
    back_two = window(density, 0, faces, along)
    here = window(density, 1, faces, along)
    ahead = window(density, 2, faces, along)
    ahead_two = window(density, 3, faces, along)
    face_speed = 0.5 * (window(velocity, 1, faces, along) + window(velocity, 2, faces, along))
    flux = jnp.maximum(face_speed, 0.0) * (1.5 * here - 0.5 * back_two) + jnp.minimum(
        face_speed, 0.0
    ) * (1.5 * ahead - 0.5 * ahead_two)
    return window(flux, 1, faces - 1, along) - window(flux, 0, faces - 1, along)


def moved(fluid, step_time):
    density = fluid[0]
    radial = fluid[1]
    azimuth = fluid[2]
    div_azimuth = face_divergence(density, azimuth, 1)
    inner_density = density[:, 2:-2]
    inner_radial = radial[:, 2:-2]
    zero_pad = ((0, 0), (0, 0), (2, 2))
    div_radial = face_divergence(
        jnp.pad(inner_density, zero_pad), jnp.pad(inner_radial, zero_pad), 2
    )
    new_density = inner_density - step_time * (div_azimuth + div_radial)
    gas_density = density[-1]
    inner_gas = gas_density[2:-2]
    grad_azimuth = 0.5 * (gas_density[3:-1] - gas_density[1:-3])
    edge_gas = jnp.pad(inner_gas, ((0, 0), (1, 1)), mode="edge")
    grad_radial = 0.5 * (edge_gas[:, 2:] - edge_gas[:, :-2])
    push = step_time * sound_sq / inner_gas
    gas_velocity = jnp.stack(
        [inner_radial[-1] - push * grad_radial, azimuth[-1, 2:-2] - push * grad_azimuth]
    )
    dust_velocity = jnp.stack([inner_radial[:-1], azimuth[:-1, 2:-2]])
    return (new_density, gas_velocity, dust_velocity)


def drag_terms(new_density, dust_velocity, stop_times, step_time, total_species):
    gas_new = new_density[-1]
    rate = step_time * gas_new[None] / stop_times[:, None, None]
    weight = new_density[:-1] / (total_species * gas_new[None]) * rate / (1.0 + rate)
    terms = jnp.stack(
        [
            jnp.sum(weight, 0),
            jnp.sum(weight * dust_velocity[0], 0),
            jnp.sum(weight * dust_velocity[1], 0),
        ]
    )
    return (rate, terms)


def coupled_gas(gas_velocity, totals):
    return (gas_velocity + totals[1:]) / (1.0 + totals[0])


def assemble(new_density, dust_velocity, gas_next, rate):
    dust_next = (dust_velocity + rate[None] * gas_next[:, None]) / (1.0 + rate[None])
    radial = jnp.concatenate([dust_next[0], gas_next[0][None]], axis=0)
    azimuth = jnp.concatenate([dust_next[1], gas_next[1][None]], axis=0)
    return jnp.stack([new_density, radial, azimuth])


def xor_pairs(count, bit):
    return [(i, i ^ bit) for i in range(count)]


def butterfly_max(value, axes):
    for axis in axes:
        count = lax.axis_size(axis)
        bit = 1
        while bit < count:
            value = jnp.maximum(value, lax.ppermute(value, axis, xor_pairs(count, bit)))
            bit *= 2
    return value


def halving_sum(block, axis):
    count = lax.axis_size(axis)
    index = lax.axis_index(axis)
    rows, lanes = block.shape
    part = block
    bits = []
    bit = 1
    while bit < count:
        dim = 0 if part.shape[0] % 2 == 0 and part.shape[0] >= 16 else 1
        half = part.shape[dim] // 2
        low = lax.slice_in_dim(part, 0, half, axis=dim)
        high = lax.slice_in_dim(part, half, None, axis=dim)
        upper = (index // bit) % 2 == 1
        keep = jnp.where(upper, high, low)
        send = jnp.where(upper, low, high)
        part = keep + lax.ppermute(send, axis, xor_pairs(count, bit))
        bits.append((bit, dim))
        bit *= 2
    for bit, dim in reversed(bits):
        other = lax.ppermute(part, axis, xor_pairs(count, bit))
        upper = (index // bit) % 2 == 1
        part = jnp.where(
            upper,
            jnp.concatenate([other, part], axis=dim),
            jnp.concatenate([part, other], axis=dim),
        )
    return part


def advance(wide, margin, tile_rows, stop_times, total_species):
    interior = lax.slice_in_dim(wide, margin, margin + tile_rows, axis=2)
    local_top = jnp.max(jnp.abs(interior[1]) + jnp.abs(interior[2]))
    fastest = butterfly_max(jnp.broadcast_to(local_top, (8, 128)), ("species", "space"))[0, 0]
    step_time = courant / (sound_speed + fastest)
    new_density, gas_velocity, dust_velocity = moved(wide, step_time)
    rate, terms = drag_terms(new_density, dust_velocity, stop_times, step_time, total_species)
    shape = terms.shape
    totals = halving_sum(terms.reshape(-1, shape[-1]), "species").reshape(shape)
    gas_next = coupled_gas(gas_velocity, totals)
    return assemble(new_density, dust_velocity, gas_next, rate)


def local(dust_state, gas_state, species_bin):
    local_species = dust_state.shape[1]
    total_species = local_species * lax.axis_size("species")
    tile_rows = dust_state.shape[2]
    fluid = jnp.concatenate([dust_state, gas_state[:, None]], axis=1)
    stop_times = stop_floor * jnp.exp(
        stop_span * species_bin.astype(jnp.float32) / (total_species - 1)
    )
    for iteration in range(STEPS):
        wide = padded(fluid, (("space", 2),), 2)
        fluid = advance(wide, 2, tile_rows, stop_times, total_species)
    return (fluid[:, :local_species], fluid[:, local_species])


def solution(mesh):
    placed = (P(None, "species", "space", None), P(None, "space", None), P("species"))
    return jax.shard_map(
        local,
        mesh=mesh,
        in_specs=placed,
        out_specs=(P(None, "species", "space", None), P(None, "space", None)),
        check_vma=False,
    )
```

```python
import jax
import jax.numpy as jnp
from jax import lax
from jax.sharding import PartitionSpec as P

STEPS = 2


courant = 0.25
sound_speed = 1.0
sound_sq = 1.0
stop_floor = 0.003
stop_span = 6.907755


def padded(block, sides, width):
    for axis, dim in sides:
        count = lax.axis_size(axis)
        forward = [(i, i + 1) for i in range(count - 1)]
        forward.append((count - 1, 0))
        backward = [(target, source) for source, target in forward]
        low = lax.ppermute(
            lax.slice_in_dim(block, block.shape[dim] - width, None, axis=dim), axis, forward
        )
        high = lax.ppermute(lax.slice_in_dim(block, 0, width, axis=dim), axis, backward)
        block = jnp.concatenate([low, block, high], axis=dim)
    return block


def window(values, start, length, along):
    return lax.slice_in_dim(values, start, start + length, axis=along)


def face_divergence(density, velocity, along):
    faces = density.shape[along] - 3
    back_two = window(density, 0, faces, along)
    here = window(density, 1, faces, along)
    ahead = window(density, 2, faces, along)
    ahead_two = window(density, 3, faces, along)
    face_speed = 0.5 * (window(velocity, 1, faces, along) + window(velocity, 2, faces, along))
    flux = jnp.maximum(face_speed, 0.0) * (1.5 * here - 0.5 * back_two) + jnp.minimum(
        face_speed, 0.0
    ) * (1.5 * ahead - 0.5 * ahead_two)
    return window(flux, 1, faces - 1, along) - window(flux, 0, faces - 1, along)


def moved(fluid, step_time):
    density = fluid[0]
    radial = fluid[1]
    azimuth = fluid[2]
    div_azimuth = face_divergence(density, azimuth, 1)
    inner_density = density[:, 2:-2]
    inner_radial = radial[:, 2:-2]
    zero_pad = ((0, 0), (0, 0), (2, 2))
    div_radial = face_divergence(
        jnp.pad(inner_density, zero_pad), jnp.pad(inner_radial, zero_pad), 2
    )
    new_density = inner_density - step_time * (div_azimuth + div_radial)
    gas_density = density[-1]
    inner_gas = gas_density[2:-2]
    grad_azimuth = 0.5 * (gas_density[3:-1] - gas_density[1:-3])
    edge_gas = jnp.pad(inner_gas, ((0, 0), (1, 1)), mode="edge")
    grad_radial = 0.5 * (edge_gas[:, 2:] - edge_gas[:, :-2])
    push = step_time * sound_sq / inner_gas
    gas_velocity = jnp.stack(
        [inner_radial[-1] - push * grad_radial, azimuth[-1, 2:-2] - push * grad_azimuth]
    )
    dust_velocity = jnp.stack([inner_radial[:-1], azimuth[:-1, 2:-2]])
    return (new_density, gas_velocity, dust_velocity)


def drag_terms(new_density, dust_velocity, stop_times, step_time, total_species):
    gas_new = new_density[-1]
    rate = step_time * gas_new[None] / stop_times[:, None, None]
    weight = new_density[:-1] / (total_species * gas_new[None]) * rate / (1.0 + rate)
    terms = jnp.stack(
        [
            jnp.sum(weight, 0),
            jnp.sum(weight * dust_velocity[0], 0),
            jnp.sum(weight * dust_velocity[1], 0),
        ]
    )
    return (rate, terms)


def coupled_gas(gas_velocity, totals):
    return (gas_velocity + totals[1:]) / (1.0 + totals[0])


def assemble(new_density, dust_velocity, gas_next, rate):
    dust_next = (dust_velocity + rate[None] * gas_next[:, None]) / (1.0 + rate[None])
    radial = jnp.concatenate([dust_next[0], gas_next[0][None]], axis=0)
    azimuth = jnp.concatenate([dust_next[1], gas_next[1][None]], axis=0)
    return jnp.stack([new_density, radial, azimuth])


def xor_pairs(count, bit):
    return [(i, i ^ bit) for i in range(count)]


def mirror_pairs(count, block):
    blocks = count // block
    return [(i, (blocks - 1 - i // block) * block + i % block) for i in range(count)]


def global_max(value, axes):
    count = 1
    for axis in axes:
        count *= lax.axis_size(axis)
    spread = jnp.broadcast_to(value, (count, 128))
    return jnp.max(lax.all_to_all(spread, axes, 0, 0, tiled=True))


def split_rounds(part, axis, rounds):
    index = lax.axis_index(axis)
    done = []
    for bit in rounds:
        dim = 0 if part.shape[0] % 2 == 0 and part.shape[0] >= 16 else 1
        half = part.shape[dim] // 2
        low = lax.slice_in_dim(part, 0, half, axis=dim)
        high = lax.slice_in_dim(part, half, None, axis=dim)
        upper = (index // bit) % 2 == 1
        keep = jnp.where(upper, high, low)
        send = jnp.where(upper, low, high)
        part = keep + lax.ppermute(send, axis, xor_pairs(lax.axis_size(axis), bit))
        done.append((bit, dim))
    return part, done


def join_rounds(part, axis, done):
    index = lax.axis_index(axis)
    for bit, dim in reversed(done):
        other = lax.ppermute(part, axis, xor_pairs(lax.axis_size(axis), bit))
        upper = (index // bit) % 2 == 1
        part = jnp.where(
            upper,
            jnp.concatenate([other, part], axis=dim),
            jnp.concatenate([part, other], axis=dim),
        )
    return part


def species_sum(block, axis):
    count = lax.axis_size(axis)
    index = lax.axis_index(axis)
    low_bits = [bit for bit in (1, 2) if bit < count]
    part, done = split_rounds(block, axis, low_bits)
    block_size = 2 * low_bits[-1] if low_bits else 1
    bit = block_size
    while bit < count:
        pairs = mirror_pairs(count, block_size) if 2 * bit >= count else xor_pairs(count, bit)
        other = lax.ppermute(part, axis, pairs)
        upper = (index // bit) % 2 == 1 if 2 * bit < count else index >= count // 2
        part = jnp.where(upper, other + part, part + other)
        bit *= 2
    return join_rounds(part, axis, done)


def advance(wide, margin, tile_rows, stop_times, total_species):
    interior = lax.slice_in_dim(wide, margin, margin + tile_rows, axis=2)
    local_top = jnp.max(jnp.abs(interior[1]) + jnp.abs(interior[2]))
    fastest = global_max(local_top, ("space", "species"))
    step_time = courant / (sound_speed + fastest)
    new_density, gas_velocity, dust_velocity = moved(wide, step_time)
    rate, terms = drag_terms(new_density, dust_velocity, stop_times, step_time, total_species)
    shape = terms.shape
    totals = species_sum(terms.reshape(-1, shape[-1]), "species").reshape(shape)
    gas_next = coupled_gas(gas_velocity, totals)
    return assemble(new_density, dust_velocity, gas_next, rate)


def local(dust_state, gas_state, species_bin):
    local_species = dust_state.shape[1]
    total_species = local_species * lax.axis_size("species")
    tile_rows = dust_state.shape[2]
    fluid = jnp.concatenate([dust_state, gas_state[:, None]], axis=1)
    stop_times = stop_floor * jnp.exp(
        stop_span * species_bin.astype(jnp.float32) / (total_species - 1)
    )
    for iteration in range(STEPS):
        wide = padded(fluid, (("space", 2),), 2)
        fluid = advance(wide, 2, tile_rows, stop_times, total_species)
    return (fluid[:, :local_species], fluid[:, local_species])


def solution(mesh):
    placed = (P(None, "species", "space", None), P(None, "space", None), P("species"))
    return jax.shard_map(
        local,
        mesh=mesh,
        in_specs=placed,
        out_specs=(P(None, "species", "space", None), P(None, "space", None)),
        check_vma=False,
    )
```

```python
import jax
import jax.numpy as jnp
from jax import lax
from jax.sharding import PartitionSpec as P

STEPS = 2


courant = 0.25
sound_speed = 1.0
sound_sq = 1.0
stop_floor = 0.003
stop_span = 6.907755


def padded(block, sides, width):
    for axis, dim in sides:
        count = lax.axis_size(axis)
        forward = [(i, i + 1) for i in range(count - 1)]
        forward.append((count - 1, 0))
        backward = [(target, source) for source, target in forward]
        low = lax.ppermute(
            lax.slice_in_dim(block, block.shape[dim] - width, None, axis=dim), axis, forward
        )
        high = lax.ppermute(lax.slice_in_dim(block, 0, width, axis=dim), axis, backward)
        block = jnp.concatenate([low, block, high], axis=dim)
    return block


def window(values, start, length, along):
    return lax.slice_in_dim(values, start, start + length, axis=along)


def face_divergence(density, velocity, along):
    faces = density.shape[along] - 3
    back_two = window(density, 0, faces, along)
    here = window(density, 1, faces, along)
    ahead = window(density, 2, faces, along)
    ahead_two = window(density, 3, faces, along)
    face_speed = 0.5 * (window(velocity, 1, faces, along) + window(velocity, 2, faces, along))
    flux = jnp.maximum(face_speed, 0.0) * (1.5 * here - 0.5 * back_two) + jnp.minimum(
        face_speed, 0.0
    ) * (1.5 * ahead - 0.5 * ahead_two)
    return window(flux, 1, faces - 1, along) - window(flux, 0, faces - 1, along)


def moved(fluid, step_time):
    density = fluid[0]
    radial = fluid[1]
    azimuth = fluid[2]
    div_azimuth = face_divergence(density, azimuth, 1)
    inner_density = density[:, 2:-2]
    inner_radial = radial[:, 2:-2]
    zero_pad = ((0, 0), (0, 0), (2, 2))
    div_radial = face_divergence(
        jnp.pad(inner_density, zero_pad), jnp.pad(inner_radial, zero_pad), 2
    )
    new_density = inner_density - step_time * (div_azimuth + div_radial)
    gas_density = density[-1]
    inner_gas = gas_density[2:-2]
    grad_azimuth = 0.5 * (gas_density[3:-1] - gas_density[1:-3])
    edge_gas = jnp.pad(inner_gas, ((0, 0), (1, 1)), mode="edge")
    grad_radial = 0.5 * (edge_gas[:, 2:] - edge_gas[:, :-2])
    push = step_time * sound_sq / inner_gas
    gas_velocity = jnp.stack(
        [inner_radial[-1] - push * grad_radial, azimuth[-1, 2:-2] - push * grad_azimuth]
    )
    dust_velocity = jnp.stack([inner_radial[:-1], azimuth[:-1, 2:-2]])
    return (new_density, gas_velocity, dust_velocity)


def drag_terms(new_density, dust_velocity, stop_times, step_time, total_species):
    gas_new = new_density[-1]
    rate = step_time * gas_new[None] / stop_times[:, None, None]
    weight = new_density[:-1] / (total_species * gas_new[None]) * rate / (1.0 + rate)
    terms = jnp.stack(
        [
            jnp.sum(weight, 0),
            jnp.sum(weight * dust_velocity[0], 0),
            jnp.sum(weight * dust_velocity[1], 0),
        ]
    )
    return (rate, terms)


def coupled_gas(gas_velocity, totals):
    return (gas_velocity + totals[1:]) / (1.0 + totals[0])


def assemble(new_density, dust_velocity, gas_next, rate):
    dust_next = (dust_velocity + rate[None] * gas_next[:, None]) / (1.0 + rate[None])
    dust = jnp.concatenate([new_density[None, :-1], dust_next], axis=0)
    gas = jnp.concatenate([new_density[None, -1], gas_next], axis=0)
    return dust, gas


def xor_pairs(count, bit):
    return [(i, i ^ bit) for i in range(count)]


def mirror_pairs(count, block):
    blocks = count // block
    return [(i, (blocks - 1 - i // block) * block + i % block) for i in range(count)]


def global_max(value, axes):
    count = 1
    for axis in axes:
        count *= lax.axis_size(axis)
    spread = jnp.broadcast_to(value, (count,))
    return jnp.max(lax.all_to_all(spread, axes, 0, 0, tiled=True))


def split_rounds(part, axis, rounds):
    index = lax.axis_index(axis)
    done = []
    for bit in rounds:
        dim = 0 if part.shape[0] % 2 == 0 and part.shape[0] >= 16 else 1
        half = part.shape[dim] // 2
        low = lax.slice_in_dim(part, 0, half, axis=dim)
        high = lax.slice_in_dim(part, half, None, axis=dim)
        upper = (index // bit) % 2 == 1
        keep = jnp.where(upper, high, low)
        send = jnp.where(upper, low, high)
        part = keep + lax.ppermute(send, axis, xor_pairs(lax.axis_size(axis), bit))
        done.append((bit, dim))
    return part, done


def join_rounds(part, axis, done):
    index = lax.axis_index(axis)
    for bit, dim in reversed(done):
        other = lax.ppermute(part, axis, xor_pairs(lax.axis_size(axis), bit))
        upper = (index // bit) % 2 == 1
        part = jnp.where(
            upper,
            jnp.concatenate([other, part], axis=dim),
            jnp.concatenate([part, other], axis=dim),
        )
    return part


def species_sum(block, axis):
    count = lax.axis_size(axis)
    index = lax.axis_index(axis)
    low_bits = [bit for bit in (1, 2) if bit < count]
    part, done = split_rounds(block, axis, low_bits)
    block_size = 2 * low_bits[-1] if low_bits else 1
    bit = block_size
    while bit < count:
        pairs = mirror_pairs(count, block_size) if 2 * bit >= count else xor_pairs(count, bit)
        other = lax.ppermute(part, axis, pairs)
        upper = (index // bit) % 2 == 1 if 2 * bit < count else index >= count // 2
        part = jnp.where(upper, other + part, part + other)
        bit *= 2
    return join_rounds(part, axis, done)


def advance(wide, margin, tile_rows, stop_times, total_species):
    interior = lax.slice_in_dim(wide, margin, margin + tile_rows, axis=2)
    local_top = jnp.max(jnp.abs(interior[1]) + jnp.abs(interior[2]))
    fastest = global_max(local_top, ("space", "species"))
    step_time = courant / (sound_speed + fastest)
    new_density, gas_velocity, dust_velocity = moved(wide, step_time)
    rate, terms = drag_terms(new_density, dust_velocity, stop_times, step_time, total_species)
    shape = terms.shape
    totals = species_sum(terms.reshape(-1, shape[-1]), "species").reshape(shape)
    gas_next = coupled_gas(gas_velocity, totals)
    return assemble(new_density, dust_velocity, gas_next, rate)


def local(dust_state, gas_state, species_bin):
    local_species = dust_state.shape[1]
    total_species = local_species * lax.axis_size("species")
    tile_rows = dust_state.shape[2]
    fluid = jnp.concatenate([dust_state, gas_state[:, None]], axis=1)
    stop_times = stop_floor * jnp.exp(
        stop_span * species_bin.astype(jnp.float32) / (total_species - 1)
    )
    for iteration in range(STEPS):
        wide = padded(fluid, (("space", 2),), 2)
        dust, gas = advance(wide, 2, tile_rows, stop_times, total_species)
        fluid = jnp.concatenate([dust, gas[:, None]], axis=1)
    return (dust, gas)


def solution(mesh):
    placed = (P(None, "species", "space", None), P(None, "space", None), P("species"))
    return jax.shard_map(
        local,
        mesh=mesh,
        in_specs=placed,
        out_specs=(P(None, "species", "space", None), P(None, "space", None)),
        check_vma=False,
    )
```

```python
import jax
import jax.numpy as jnp
from jax import lax
from jax.experimental import pallas as pl
from jax.experimental.pallas import tpu as pltpu
from jax.sharding import PartitionSpec as P

STEPS = 2


courant = 0.25
sound_speed = 1.0
sound_sq = 1.0
stop_floor = 0.003
stop_span = 6.907755


def padded(block, sides, width):
    for axis, dim in sides:
        count = lax.axis_size(axis)
        forward = [(i, i + 1) for i in range(count - 1)]
        forward.append((count - 1, 0))
        backward = [(target, source) for source, target in forward]
        low = lax.ppermute(
            lax.slice_in_dim(block, block.shape[dim] - width, None, axis=dim), axis, forward
        )
        high = lax.ppermute(lax.slice_in_dim(block, 0, width, axis=dim), axis, backward)
        block = jnp.concatenate([low, block, high], axis=dim)
    return block


def window(values, start, length, along):
    return lax.slice_in_dim(values, start, start + length, axis=along)


def face_divergence(density, velocity, along):
    faces = density.shape[along] - 3
    back_two = window(density, 0, faces, along)
    here = window(density, 1, faces, along)
    ahead = window(density, 2, faces, along)
    ahead_two = window(density, 3, faces, along)
    face_speed = 0.5 * (window(velocity, 1, faces, along) + window(velocity, 2, faces, along))
    flux = jnp.maximum(face_speed, 0.0) * (1.5 * here - 0.5 * back_two) + jnp.minimum(
        face_speed, 0.0
    ) * (1.5 * ahead - 0.5 * ahead_two)
    return window(flux, 1, faces - 1, along) - window(flux, 0, faces - 1, along)


def moved(fluid, step_time):
    density = fluid[0]
    radial = fluid[1]
    azimuth = fluid[2]
    div_azimuth = face_divergence(density, azimuth, 1)
    inner_density = density[:, 2:-2]
    inner_radial = radial[:, 2:-2]
    zero_pad = ((0, 0), (0, 0), (2, 2))
    div_radial = face_divergence(
        jnp.pad(inner_density, zero_pad), jnp.pad(inner_radial, zero_pad), 2
    )
    new_density = inner_density - step_time * (div_azimuth + div_radial)
    gas_density = density[-1]
    inner_gas = gas_density[2:-2]
    grad_azimuth = 0.5 * (gas_density[3:-1] - gas_density[1:-3])
    edge_gas = jnp.pad(inner_gas, ((0, 0), (1, 1)), mode="edge")
    grad_radial = 0.5 * (edge_gas[:, 2:] - edge_gas[:, :-2])
    push = step_time * sound_sq / inner_gas
    gas_velocity = jnp.stack(
        [inner_radial[-1] - push * grad_radial, azimuth[-1, 2:-2] - push * grad_azimuth]
    )
    dust_velocity = jnp.stack([inner_radial[:-1], azimuth[:-1, 2:-2]])
    return (new_density, gas_velocity, dust_velocity)


def drag_terms(new_density, dust_velocity, stop_times, step_time, total_species):
    gas_new = new_density[-1]
    rate = step_time * gas_new[None] / stop_times[:, None, None]
    weight = new_density[:-1] / (total_species * gas_new[None]) * rate / (1.0 + rate)
    terms = jnp.stack(
        [
            jnp.sum(weight, 0),
            jnp.sum(weight * dust_velocity[0], 0),
            jnp.sum(weight * dust_velocity[1], 0),
        ]
    )
    return (rate, terms)


def coupled_gas(gas_velocity, totals):
    return (gas_velocity + totals[1:]) / (1.0 + totals[0])


def assemble(new_density, dust_velocity, gas_next, rate):
    dust_next = (dust_velocity + rate[None] * gas_next[:, None]) / (1.0 + rate[None])
    dust = jnp.concatenate([new_density[None, :-1], dust_next], axis=0)
    gas = jnp.concatenate([new_density[None, -1], gas_next], axis=0)
    return dust, gas


def xor_pairs(count, bit):
    return [(i, i ^ bit) for i in range(count)]


def mirror_pairs(count, block):
    blocks = count // block
    return [(i, (blocks - 1 - i // block) * block + i % block) for i in range(count)]


def global_max(value, axes):
    count = 1
    for axis in axes:
        count *= lax.axis_size(axis)
    spread = jnp.broadcast_to(value, (count,))
    return jnp.max(lax.all_to_all(spread, axes, 0, 0, tiled=True))


def split_rounds(part, axis, rounds):
    index = lax.axis_index(axis)
    done = []
    for bit in rounds:
        dim = 0 if part.shape[0] % 2 == 0 and part.shape[0] >= 16 else 1
        half = part.shape[dim] // 2
        low = lax.slice_in_dim(part, 0, half, axis=dim)
        high = lax.slice_in_dim(part, half, None, axis=dim)
        upper = (index // bit) % 2 == 1
        keep = jnp.where(upper, high, low)
        send = jnp.where(upper, low, high)
        part = keep + lax.ppermute(send, axis, xor_pairs(lax.axis_size(axis), bit))
        done.append((bit, dim))
    return part, done


def join_rounds(part, axis, done):
    index = lax.axis_index(axis)
    for bit, dim in reversed(done):
        other = lax.ppermute(part, axis, xor_pairs(lax.axis_size(axis), bit))
        upper = (index // bit) % 2 == 1
        part = jnp.where(
            upper,
            jnp.concatenate([other, part], axis=dim),
            jnp.concatenate([part, other], axis=dim),
        )
    return part


def species_sum(block, axis, first_done=()):
    count = lax.axis_size(axis)
    index = lax.axis_index(axis)
    low_bits = [bit for bit in (1, 2) if bit < count]
    taken = [bit for bit, dim in first_done]
    part, done = split_rounds(block, axis, [bit for bit in low_bits if bit not in taken])
    done = list(first_done) + done
    block_size = 2 * low_bits[-1] if low_bits else 1
    bit = block_size
    while bit < count:
        pairs = mirror_pairs(count, block_size) if 2 * bit >= count else xor_pairs(count, bit)
        other = lax.ppermute(part, axis, pairs)
        upper = (index // bit) % 2 == 1 if 2 * bit < count else index >= count // 2
        part = jnp.where(upper, other + part, part + other)
        bit *= 2
    return join_rounds(part, axis, done)


def drag_kernel(scalars, stop_times, flag, dust, gas, divergence, density_out, keep, send):
    step_time = scalars[0]
    total_species = scalars[1]
    local_species = dust.shape[1]
    gas_new = gas[0] - step_time * divergence[local_species]
    density_out[local_species] = gas_new
    scale = total_species * gas_new
    sums = [None, None, None]
    for k in range(local_species):
        fresh = dust[0, k] - step_time * divergence[k]
        density_out[k] = fresh
        rate = step_time * gas_new / stop_times[k]
        weight = fresh / scale * rate / (1.0 + rate)
        parts = (weight, weight * dust[1, k], weight * dust[2, k])
        sums = [p if s is None else s + p for s, p in zip(sums, parts)]
    rows = gas_new.shape[0]
    half = rows // 2
    total_zero, total_radial, total_azimuth = sums

    @pl.when(flag[0] == 0)
    def _():
        keep[0:rows] = total_zero
        keep[rows : rows + half] = total_radial[0:half]
        send[0:half] = total_radial[half:rows]
        send[half : half + rows] = total_azimuth

    @pl.when(flag[0] != 0)
    def _():
        send[0:rows] = total_zero
        send[rows : rows + half] = total_radial[0:half]
        keep[0:half] = total_radial[half:rows]
        keep[half : half + rows] = total_azimuth


def update_kernel(scalars, stop_times, totals, gas_star, density, dust, dust_out, gas_out, top):
    step_time = scalars[0]
    local_species = dust.shape[1]
    rows = gas_star.shape[1]
    gas_new = density[local_species]
    relief = 1.0 + totals[0:rows]
    gas_radial = (gas_star[0] + totals[rows : 2 * rows]) / relief
    gas_azimuth = (gas_star[1] + totals[2 * rows : 3 * rows]) / relief
    gas_out[0] = gas_new
    gas_out[1] = gas_radial
    gas_out[2] = gas_azimuth
    fastest = jnp.abs(gas_radial) + jnp.abs(gas_azimuth)
    for k in range(local_species):
        rate = step_time * gas_new / stop_times[k]
        radial = (dust[1, k] + rate * gas_radial) / (1.0 + rate)
        azimuth = (dust[2, k] + rate * gas_azimuth) / (1.0 + rate)
        dust_out[0, k] = density[k]
        dust_out[1, k] = radial
        dust_out[2, k] = azimuth
        fastest = jnp.maximum(fastest, jnp.abs(radial) + jnp.abs(azimuth))
    top[...] = jnp.broadcast_to(jnp.max(fastest, axis=0, keepdims=True), top.shape)


def smem():
    return pl.BlockSpec(memory_space=pltpu.SMEM)


def vmem():
    return pl.BlockSpec(memory_space=pltpu.VMEM)


def drag_call(scalars, stop_times, flag, dust, gas, divergence):
    rows, lanes = gas.shape[1:]
    f32 = jnp.float32
    return pl.pallas_call(
        drag_kernel,
        out_shape=(
            jax.ShapeDtypeStruct(divergence.shape, f32),
            jax.ShapeDtypeStruct((3 * rows // 2, lanes), f32),
            jax.ShapeDtypeStruct((3 * rows // 2, lanes), f32),
        ),
        in_specs=[smem(), smem(), smem(), vmem(), vmem(), vmem()],
        out_specs=(vmem(), vmem(), vmem()),
    )(scalars, stop_times, flag, dust, gas, divergence)


def update_call(scalars, stop_times, totals, gas_star, density, dust):
    f32 = jnp.float32
    return pl.pallas_call(
        update_kernel,
        out_shape=(
            jax.ShapeDtypeStruct(dust.shape, f32),
            jax.ShapeDtypeStruct((3,) + gas_star.shape[1:], f32),
            jax.ShapeDtypeStruct((8, gas_star.shape[2]), f32),
        ),
        in_specs=[smem(), smem(), vmem(), vmem(), vmem(), vmem()],
        out_specs=(vmem(), vmem(), vmem()),
    )(scalars, stop_times, totals, gas_star, density, dust)


def transport(wide):
    density = wide[0]
    radial = wide[1]
    azimuth = wide[2]
    div_azimuth = face_divergence(density, azimuth, 1)
    inner_density = density[:, 2:-2]
    inner_radial = radial[:, 2:-2]
    zero_pad = ((0, 0), (0, 0), (2, 2))
    div_radial = face_divergence(
        jnp.pad(inner_density, zero_pad), jnp.pad(inner_radial, zero_pad), 2
    )
    gas_density = density[-1]
    inner_gas = gas_density[2:-2]
    grad_azimuth = 0.5 * (gas_density[3:-1] - gas_density[1:-3])
    edge_gas = jnp.pad(inner_gas, ((0, 0), (1, 1)), mode="edge")
    grad_radial = 0.5 * (edge_gas[:, 2:] - edge_gas[:, :-2])
    return div_azimuth + div_radial, inner_gas, grad_radial, grad_azimuth


def advance(wide, dust, gas, local_top, stop_times, total_species):
    divergence, inner_gas, grad_radial, grad_azimuth = transport(wide)
    fastest = global_max(local_top, ("space", "species"))
    step_time = courant / (sound_speed + fastest)
    scalars = jnp.stack([step_time, jnp.float32(total_species)])
    flag = (lax.axis_index("species") % 2).astype(jnp.int32).reshape(1)
    density, keep, send = drag_call(scalars, stop_times, flag, dust, gas, divergence)
    push = step_time * sound_sq / inner_gas
    gas_star = jnp.stack([gas[1] - push * grad_radial, gas[2] - push * grad_azimuth])
    part = keep + lax.ppermute(send, "species", xor_pairs(lax.axis_size("species"), 1))
    totals = species_sum(part, "species", first_done=[(1, 0)])
    return update_call(scalars, stop_times, totals, gas_star, density, dust)


def local(dust_state, gas_state, species_bin):
    local_species = dust_state.shape[1]
    total_species = local_species * lax.axis_size("species")
    stop_times = stop_floor * jnp.exp(
        stop_span * species_bin.astype(jnp.float32) / (total_species - 1)
    )
    dust, gas = dust_state, gas_state
    local_top = jnp.maximum(
        jnp.max(jnp.abs(dust[1]) + jnp.abs(dust[2])), jnp.max(jnp.abs(gas[1]) + jnp.abs(gas[2]))
    )
    for iteration in range(STEPS):
        fluid = jnp.concatenate([dust, gas[:, None]], axis=1)
        wide = padded(fluid, (("space", 2),), 2)
        dust, gas, top = advance(wide, dust, gas, local_top, stop_times, total_species)
        local_top = jnp.max(top)
    return (dust, gas)


def solution(mesh):
    placed = (P(None, "species", "space", None), P(None, "space", None), P("species"))
    return jax.shard_map(
        local,
        mesh=mesh,
        in_specs=placed,
        out_specs=(P(None, "species", "space", None), P(None, "space", None)),
        check_vma=False,
    )
```

```python
import jax
import jax.numpy as jnp
from jax import lax
from jax.sharding import PartitionSpec as P

STEPS = 2


courant = 0.25
sound_speed = 1.0
sound_sq = 1.0
stop_floor = 0.003
stop_span = 6.907755


def padded(block, sides, width):
    for axis, dim in sides:
        count = lax.axis_size(axis)
        forward = [(i, i + 1) for i in range(count - 1)]
        forward.append((count - 1, 0))
        backward = [(target, source) for source, target in forward]
        low = lax.ppermute(
            lax.slice_in_dim(block, block.shape[dim] - width, None, axis=dim), axis, forward
        )
        high = lax.ppermute(lax.slice_in_dim(block, 0, width, axis=dim), axis, backward)
        block = jnp.concatenate([low, block, high], axis=dim)
    return block


def window(values, start, length, along):
    return lax.slice_in_dim(values, start, start + length, axis=along)


def face_divergence(density, velocity, along):
    faces = density.shape[along] - 3
    back_two = window(density, 0, faces, along)
    here = window(density, 1, faces, along)
    ahead = window(density, 2, faces, along)
    ahead_two = window(density, 3, faces, along)
    face_speed = 0.5 * (window(velocity, 1, faces, along) + window(velocity, 2, faces, along))
    flux = jnp.maximum(face_speed, 0.0) * (1.5 * here - 0.5 * back_two) + jnp.minimum(
        face_speed, 0.0
    ) * (1.5 * ahead - 0.5 * ahead_two)
    return window(flux, 1, faces - 1, along) - window(flux, 0, faces - 1, along)


def moved(fluid, step_time):
    density = fluid[0]
    radial = fluid[1]
    azimuth = fluid[2]
    div_azimuth = face_divergence(density, azimuth, 1)
    inner_density = density[:, 2:-2]
    inner_radial = radial[:, 2:-2]
    zero_pad = ((0, 0), (0, 0), (2, 2))
    div_radial = face_divergence(
        jnp.pad(inner_density, zero_pad), jnp.pad(inner_radial, zero_pad), 2
    )
    new_density = inner_density - step_time * (div_azimuth + div_radial)
    gas_density = density[-1]
    inner_gas = gas_density[2:-2]
    grad_azimuth = 0.5 * (gas_density[3:-1] - gas_density[1:-3])
    edge_gas = jnp.pad(inner_gas, ((0, 0), (1, 1)), mode="edge")
    grad_radial = 0.5 * (edge_gas[:, 2:] - edge_gas[:, :-2])
    push = step_time * sound_sq / inner_gas
    gas_velocity = jnp.stack(
        [inner_radial[-1] - push * grad_radial, azimuth[-1, 2:-2] - push * grad_azimuth]
    )
    dust_velocity = jnp.stack([inner_radial[:-1], azimuth[:-1, 2:-2]])
    return (new_density, gas_velocity, dust_velocity)


def drag_terms(new_density, dust_velocity, stop_times, step_time, total_species):
    gas_new = new_density[-1]
    rate = step_time * gas_new[None] / stop_times[:, None, None]
    weight = new_density[:-1] / (total_species * gas_new[None]) * rate / (1.0 + rate)
    terms = jnp.stack(
        [
            jnp.sum(weight, 0),
            jnp.sum(weight * dust_velocity[0], 0),
            jnp.sum(weight * dust_velocity[1], 0),
        ]
    )
    return (rate, terms)


def coupled_gas(gas_velocity, totals):
    return (gas_velocity + totals[1:]) / (1.0 + totals[0])


def assemble(new_density, dust_velocity, gas_next, rate):
    dust_next = (dust_velocity + rate[None] * gas_next[:, None]) / (1.0 + rate[None])
    dust = jnp.concatenate([new_density[None, :-1], dust_next], axis=0)
    gas = jnp.concatenate([new_density[None, -1], gas_next], axis=0)
    return dust, gas


def xor_pairs(count, bit):
    return [(i, i ^ bit) for i in range(count)]


def mirror_pairs(count, block):
    blocks = count // block
    return [(i, (blocks - 1 - i // block) * block + i % block) for i in range(count)]


def global_max(value, axes):
    count = 1
    for axis in axes:
        count *= lax.axis_size(axis)
    spread = jnp.broadcast_to(value, (count,))
    return jnp.max(lax.all_to_all(spread, axes, 0, 0, tiled=True))


def split_rounds(part, axis, rounds):
    index = lax.axis_index(axis)
    done = []
    for bit in rounds:
        dim = 0 if part.shape[0] % 2 == 0 and part.shape[0] >= 16 else 1
        half = part.shape[dim] // 2
        low = lax.slice_in_dim(part, 0, half, axis=dim)
        high = lax.slice_in_dim(part, half, None, axis=dim)
        upper = (index // bit) % 2 == 1
        keep = jnp.where(upper, high, low)
        send = jnp.where(upper, low, high)
        part = keep + lax.ppermute(send, axis, xor_pairs(lax.axis_size(axis), bit))
        done.append((bit, dim))
    return part, done


def join_rounds(part, axis, done):
    index = lax.axis_index(axis)
    for bit, dim in reversed(done):
        other = lax.ppermute(part, axis, xor_pairs(lax.axis_size(axis), bit))
        upper = (index // bit) % 2 == 1
        part = jnp.where(
            upper,
            jnp.concatenate([other, part], axis=dim),
            jnp.concatenate([part, other], axis=dim),
        )
    return part


def species_sum(block, axis, first_done=()):
    count = lax.axis_size(axis)
    index = lax.axis_index(axis)
    low_bits = [bit for bit in (1, 2) if bit < count]
    taken = [bit for bit, dim in first_done]
    part, done = split_rounds(block, axis, [bit for bit in low_bits if bit not in taken])
    done = list(first_done) + done
    block_size = 2 * low_bits[-1] if low_bits else 1
    bit = block_size
    while bit < count:
        pairs = mirror_pairs(count, block_size) if 2 * bit >= count else xor_pairs(count, bit)
        other = lax.ppermute(part, axis, pairs)
        upper = (index // bit) % 2 == 1 if 2 * bit < count else index >= count // 2
        part = jnp.where(upper, other + part, part + other)
        bit *= 2
    return join_rounds(part, axis, done)


def drag_sums(step_time, stop_times, upper, dust, gas, divergence, total_species):
    local_species = dust.shape[1]
    gas_new = gas[0] - step_time * divergence[local_species]
    fresh = dust[0] - step_time * divergence[:local_species]
    rate = step_time * gas_new[None] / stop_times[:, None, None]
    weight = fresh / (total_species * gas_new[None]) * rate / (1.0 + rate)
    totals = jnp.concatenate(
        [jnp.sum(weight, 0), jnp.sum(weight * dust[1], 0), jnp.sum(weight * dust[2], 0)], axis=0
    )
    half = totals.shape[0] // 2
    low, high = totals[:half], totals[half:]
    keep = jnp.where(upper, high, low)
    send = jnp.where(upper, low, high)
    density = jnp.concatenate([fresh, gas_new[None]], axis=0)
    return density, keep, send


def updated(step_time, stop_times, totals, gas_star, density, dust):
    local_species = dust.shape[1]
    rows = gas_star.shape[1]
    gas_new = density[local_species]
    relief = 1.0 + totals[0:rows]
    gas_velocity = jnp.stack(
        [(gas_star[0] + totals[rows : 2 * rows]) / relief, (gas_star[1] + totals[2 * rows :]) / relief]
    )
    rate = step_time * gas_new[None] / stop_times[:, None, None]
    dust_velocity = (dust[1:] + rate[None] * gas_velocity[:, None]) / (1.0 + rate[None])
    dust_next = jnp.concatenate([density[None, :local_species], dust_velocity], axis=0)
    gas_next = jnp.concatenate([gas_new[None], gas_velocity], axis=0)
    speed = jnp.maximum(
        jnp.max(jnp.abs(dust_velocity[0]) + jnp.abs(dust_velocity[1])),
        jnp.max(jnp.abs(gas_velocity[0]) + jnp.abs(gas_velocity[1])),
    )
    return dust_next, gas_next, speed


def transport(wide):
    density = wide[0]
    radial = wide[1]
    azimuth = wide[2]
    div_azimuth = face_divergence(density, azimuth, 1)
    inner_density = density[:, 2:-2]
    inner_radial = radial[:, 2:-2]
    zero_pad = ((0, 0), (0, 0), (2, 2))
    div_radial = face_divergence(
        jnp.pad(inner_density, zero_pad), jnp.pad(inner_radial, zero_pad), 2
    )
    gas_density = density[-1]
    inner_gas = gas_density[2:-2]
    grad_azimuth = 0.5 * (gas_density[3:-1] - gas_density[1:-3])
    edge_gas = jnp.pad(inner_gas, ((0, 0), (1, 1)), mode="edge")
    grad_radial = 0.5 * (edge_gas[:, 2:] - edge_gas[:, :-2])
    return div_azimuth + div_radial, inner_gas, grad_radial, grad_azimuth


def advance(wide, dust, gas, local_top, stop_times, total_species):
    divergence, inner_gas, grad_radial, grad_azimuth = transport(wide)
    fastest = global_max(local_top, ("space", "species"))
    step_time = courant / (sound_speed + fastest)
    upper = lax.axis_index("species") % 2 == 1
    density, keep, send = drag_sums(step_time, stop_times, upper, dust, gas, divergence, total_species)
    push = step_time * sound_sq / inner_gas
    gas_star = jnp.stack([gas[1] - push * grad_radial, gas[2] - push * grad_azimuth])
    part = keep + lax.ppermute(send, "species", xor_pairs(lax.axis_size("species"), 1))
    totals = species_sum(part, "species", first_done=[(1, 0)])
    return updated(step_time, stop_times, totals, gas_star, density, dust)


def local(dust_state, gas_state, species_bin):
    local_species = dust_state.shape[1]
    total_species = local_species * lax.axis_size("species")
    stop_times = stop_floor * jnp.exp(
        stop_span * species_bin.astype(jnp.float32) / (total_species - 1)
    )
    dust, gas = dust_state, gas_state
    local_top = jnp.maximum(
        jnp.max(jnp.abs(dust[1]) + jnp.abs(dust[2])), jnp.max(jnp.abs(gas[1]) + jnp.abs(gas[2]))
    )
    for iteration in range(STEPS):
        fluid = jnp.concatenate([dust, gas[:, None]], axis=1)
        wide = padded(fluid, (("space", 2),), 2)
        dust, gas, local_top = advance(wide, dust, gas, local_top, stop_times, total_species)
    return (dust, gas)


def solution(mesh):
    placed = (P(None, "species", "space", None), P(None, "space", None), P("species"))
    return jax.shard_map(
        local,
        mesh=mesh,
        in_specs=placed,
        out_specs=(P(None, "species", "space", None), P(None, "space", None)),
        check_vma=False,
    )
```

```python
import jax
import jax.numpy as jnp
from jax import lax
from jax.sharding import PartitionSpec as P

STEPS = 2


courant = 0.25
sound_speed = 1.0
sound_sq = 1.0
stop_floor = 0.003
stop_span = 6.907755


def padded(block, sides, width):
    for axis, dim in sides:
        count = lax.axis_size(axis)
        forward = [(i, i + 1) for i in range(count - 1)]
        forward.append((count - 1, 0))
        backward = [(target, source) for source, target in forward]
        low = lax.ppermute(
            lax.slice_in_dim(block, block.shape[dim] - width, None, axis=dim), axis, forward
        )
        high = lax.ppermute(lax.slice_in_dim(block, 0, width, axis=dim), axis, backward)
        block = jnp.concatenate([low, block, high], axis=dim)
    return block


def window(values, start, length, along):
    return lax.slice_in_dim(values, start, start + length, axis=along)


def face_divergence(density, velocity, along):
    faces = density.shape[along] - 3
    back_two = window(density, 0, faces, along)
    here = window(density, 1, faces, along)
    ahead = window(density, 2, faces, along)
    ahead_two = window(density, 3, faces, along)
    face_speed = 0.5 * (window(velocity, 1, faces, along) + window(velocity, 2, faces, along))
    flux = jnp.maximum(face_speed, 0.0) * (1.5 * here - 0.5 * back_two) + jnp.minimum(
        face_speed, 0.0
    ) * (1.5 * ahead - 0.5 * ahead_two)
    return window(flux, 1, faces - 1, along) - window(flux, 0, faces - 1, along)


def moved(fluid, step_time):
    density = fluid[0]
    radial = fluid[1]
    azimuth = fluid[2]
    div_azimuth = face_divergence(density, azimuth, 1)
    inner_density = density[:, 2:-2]
    inner_radial = radial[:, 2:-2]
    zero_pad = ((0, 0), (0, 0), (2, 2))
    div_radial = face_divergence(
        jnp.pad(inner_density, zero_pad), jnp.pad(inner_radial, zero_pad), 2
    )
    new_density = inner_density - step_time * (div_azimuth + div_radial)
    gas_density = density[-1]
    inner_gas = gas_density[2:-2]
    grad_azimuth = 0.5 * (gas_density[3:-1] - gas_density[1:-3])
    edge_gas = jnp.pad(inner_gas, ((0, 0), (1, 1)), mode="edge")
    grad_radial = 0.5 * (edge_gas[:, 2:] - edge_gas[:, :-2])
    push = step_time * sound_sq / inner_gas
    gas_velocity = jnp.stack(
        [inner_radial[-1] - push * grad_radial, azimuth[-1, 2:-2] - push * grad_azimuth]
    )
    dust_velocity = jnp.stack([inner_radial[:-1], azimuth[:-1, 2:-2]])
    return (new_density, gas_velocity, dust_velocity)


def drag_terms(new_density, dust_velocity, stop_times, step_time, total_species):
    gas_new = new_density[-1]
    rate = step_time * gas_new[None] / stop_times[:, None, None]
    weight = new_density[:-1] / (total_species * gas_new[None]) * rate / (1.0 + rate)
    terms = jnp.stack(
        [
            jnp.sum(weight, 0),
            jnp.sum(weight * dust_velocity[0], 0),
            jnp.sum(weight * dust_velocity[1], 0),
        ]
    )
    return (rate, terms)


def coupled_gas(gas_velocity, totals):
    return (gas_velocity + totals[1:]) / (1.0 + totals[0])


def assemble(new_density, dust_velocity, gas_next, rate):
    dust_next = (dust_velocity + rate[None] * gas_next[:, None]) / (1.0 + rate[None])
    dust = jnp.concatenate([new_density[None, :-1], dust_next], axis=0)
    gas = jnp.concatenate([new_density[None, -1], gas_next], axis=0)
    return dust, gas


def xor_pairs(count, bit):
    return [(i, i ^ bit) for i in range(count)]


def mirror_pairs(count, block):
    blocks = count // block
    return [(i, (blocks - 1 - i // block) * block + i % block) for i in range(count)]


def global_max(value, axes):
    count = 1
    for axis in axes:
        count *= lax.axis_size(axis)
    spread = jnp.broadcast_to(value, (count,))
    return jnp.max(lax.all_to_all(spread, axes, 0, 0, tiled=True))


def split_rounds(part, axis, rounds):
    index = lax.axis_index(axis)
    done = []
    for bit in rounds:
        dim = 0 if part.shape[0] % 2 == 0 and part.shape[0] >= 16 else 1
        half = part.shape[dim] // 2
        low = lax.slice_in_dim(part, 0, half, axis=dim)
        high = lax.slice_in_dim(part, half, None, axis=dim)
        upper = (index // bit) % 2 == 1
        keep = jnp.where(upper, high, low)
        send = jnp.where(upper, low, high)
        part = keep + lax.ppermute(send, axis, xor_pairs(lax.axis_size(axis), bit))
        done.append((bit, dim))
    return part, done


def join_rounds(part, axis, done):
    index = lax.axis_index(axis)
    for bit, dim in reversed(done):
        other = lax.ppermute(part, axis, xor_pairs(lax.axis_size(axis), bit))
        upper = (index // bit) % 2 == 1
        part = jnp.where(
            upper,
            jnp.concatenate([other, part], axis=dim),
            jnp.concatenate([part, other], axis=dim),
        )
    return part


def species_sum(block, axis, first_done=()):
    count = lax.axis_size(axis)
    index = lax.axis_index(axis)
    low_bits = [bit for bit in (1, 2) if bit < count]
    taken = [bit for bit, dim in first_done]
    part, done = split_rounds(block, axis, [bit for bit in low_bits if bit not in taken])
    done = list(first_done) + done
    block_size = 2 * low_bits[-1] if low_bits else 1
    bit = block_size
    while bit < count:
        pairs = mirror_pairs(count, block_size) if 2 * bit >= count else xor_pairs(count, bit)
        other = lax.ppermute(part, axis, pairs)
        upper = (index // bit) % 2 == 1 if 2 * bit < count else index >= count // 2
        part = jnp.where(upper, other + part, part + other)
        bit *= 2
    return join_rounds(part, axis, done)


def drag_sums(step_time, stop_times, upper, dust, gas_density, divergence, total_species):
    local_species = dust.shape[1]
    gas_new = gas_density - step_time * divergence[local_species]
    fresh = dust[0] - step_time * divergence[:local_species]
    rate = step_time * gas_new[None] / stop_times[:, None, None]
    weight = fresh / (total_species * gas_new[None]) * rate / (1.0 + rate)
    totals = jnp.concatenate(
        [jnp.sum(weight, 0), jnp.sum(weight * dust[1], 0), jnp.sum(weight * dust[2], 0)], axis=0
    )
    half = totals.shape[0] // 2
    low, high = totals[:half], totals[half:]
    keep = jnp.where(upper, high, low)
    send = jnp.where(upper, low, high)
    density = jnp.concatenate([fresh, gas_new[None]], axis=0)
    return density, rate, keep, send


def advance(wide, margin, tile_rows, stop_times, total_species):
    interior = lax.slice_in_dim(wide, margin, margin + tile_rows, axis=2)
    local_top = jnp.max(jnp.abs(interior[1]) + jnp.abs(interior[2]))
    fastest = global_max(local_top, ("space", "species"))
    step_time = courant / (sound_speed + fastest)
    density = wide[0]
    radial = wide[1]
    azimuth = wide[2]
    div_azimuth = face_divergence(density, azimuth, 1)
    inner_density = density[:, 2:-2]
    inner_radial = radial[:, 2:-2]
    zero_pad = ((0, 0), (0, 0), (2, 2))
    div_radial = face_divergence(
        jnp.pad(inner_density, zero_pad), jnp.pad(inner_radial, zero_pad), 2
    )
    divergence = div_azimuth + div_radial
    dust = interior[:, :-1]
    upper = lax.axis_index("species") % 2 == 1
    new_density, rate, keep, send = drag_sums(
        step_time, stop_times, upper, dust, inner_density[-1], divergence, total_species
    )
    gas_density = density[-1]
    inner_gas = gas_density[2:-2]
    grad_azimuth = 0.5 * (gas_density[3:-1] - gas_density[1:-3])
    edge_gas = jnp.pad(inner_gas, ((0, 0), (1, 1)), mode="edge")
    grad_radial = 0.5 * (edge_gas[:, 2:] - edge_gas[:, :-2])
    push = step_time * sound_sq / inner_gas
    gas_velocity = jnp.stack(
        [inner_radial[-1] - push * grad_radial, azimuth[-1, 2:-2] - push * grad_azimuth]
    )
    dust_velocity = jnp.stack([inner_radial[:-1], azimuth[:-1, 2:-2]])
    part = keep + lax.ppermute(send, "species", xor_pairs(lax.axis_size("species"), 1))
    totals = species_sum(part, "species", first_done=[(1, 0)])
    totals = totals.reshape(3, tile_rows, -1)
    gas_next = coupled_gas(gas_velocity, totals)
    return assemble(new_density, dust_velocity, gas_next, rate)


def local(dust_state, gas_state, species_bin):
    local_species = dust_state.shape[1]
    total_species = local_species * lax.axis_size("species")
    tile_rows = dust_state.shape[2]
    fluid = jnp.concatenate([dust_state, gas_state[:, None]], axis=1)
    stop_times = stop_floor * jnp.exp(
        stop_span * species_bin.astype(jnp.float32) / (total_species - 1)
    )
    for iteration in range(STEPS):
        wide = padded(fluid, (("space", 2),), 2)
        dust, gas = advance(wide, 2, tile_rows, stop_times, total_species)
        fluid = jnp.concatenate([dust, gas[:, None]], axis=1)
    return (dust, gas)


def solution(mesh):
    placed = (P(None, "species", "space", None), P(None, "space", None), P("species"))
    return jax.shard_map(
        local,
        mesh=mesh,
        in_specs=placed,
        out_specs=(P(None, "species", "space", None), P(None, "space", None)),
        check_vma=False,
    )
```

```python
import jax
import jax.numpy as jnp
from jax import lax
from jax.sharding import PartitionSpec as P

STEPS = 2


courant = 0.25
sound_speed = 1.0
sound_sq = 1.0
stop_floor = 0.003
stop_span = 6.907755


def padded(block, sides, width):
    moving = jnp.stack([block[0], block[2]])
    for axis, dim in sides:
        count = lax.axis_size(axis)
        forward = [(i, i + 1) for i in range(count - 1)]
        forward.append((count - 1, 0))
        backward = [(target, source) for source, target in forward]
        low = lax.ppermute(
            lax.slice_in_dim(moving, moving.shape[dim] - width, None, axis=dim), axis, forward
        )
        high = lax.ppermute(lax.slice_in_dim(moving, 0, width, axis=dim), axis, backward)
        moving = jnp.concatenate([low, moving, high], axis=dim)
        pad = [(0, 0)] * block.ndim
        pad[dim] = (width, width)
        radial = jnp.pad(block[1], pad[1:])
        block = jnp.stack([moving[0], radial, moving[1]])
    return block


def window(values, start, length, along):
    return lax.slice_in_dim(values, start, start + length, axis=along)


def face_divergence(density, velocity, along):
    faces = density.shape[along] - 3
    back_two = window(density, 0, faces, along)
    here = window(density, 1, faces, along)
    ahead = window(density, 2, faces, along)
    ahead_two = window(density, 3, faces, along)
    face_speed = 0.5 * (window(velocity, 1, faces, along) + window(velocity, 2, faces, along))
    flux = jnp.maximum(face_speed, 0.0) * (1.5 * here - 0.5 * back_two) + jnp.minimum(
        face_speed, 0.0
    ) * (1.5 * ahead - 0.5 * ahead_two)
    return window(flux, 1, faces - 1, along) - window(flux, 0, faces - 1, along)


def moved(fluid, step_time):
    density = fluid[0]
    radial = fluid[1]
    azimuth = fluid[2]
    div_azimuth = face_divergence(density, azimuth, 1)
    inner_density = density[:, 2:-2]
    inner_radial = radial[:, 2:-2]
    zero_pad = ((0, 0), (0, 0), (2, 2))
    div_radial = face_divergence(
        jnp.pad(inner_density, zero_pad), jnp.pad(inner_radial, zero_pad), 2
    )
    new_density = inner_density - step_time * (div_azimuth + div_radial)
    gas_density = density[-1]
    inner_gas = gas_density[2:-2]
    grad_azimuth = 0.5 * (gas_density[3:-1] - gas_density[1:-3])
    edge_gas = jnp.pad(inner_gas, ((0, 0), (1, 1)), mode="edge")
    grad_radial = 0.5 * (edge_gas[:, 2:] - edge_gas[:, :-2])
    push = step_time * sound_sq / inner_gas
    gas_velocity = jnp.stack(
        [inner_radial[-1] - push * grad_radial, azimuth[-1, 2:-2] - push * grad_azimuth]
    )
    dust_velocity = jnp.stack([inner_radial[:-1], azimuth[:-1, 2:-2]])
    return (new_density, gas_velocity, dust_velocity)


def drag_terms(new_density, dust_velocity, stop_times, step_time, total_species):
    gas_new = new_density[-1]
    rate = step_time * gas_new[None] / stop_times[:, None, None]
    weight = new_density[:-1] / (total_species * gas_new[None]) * rate / (1.0 + rate)
    terms = jnp.stack(
        [
            jnp.sum(weight, 0),
            jnp.sum(weight * dust_velocity[0], 0),
            jnp.sum(weight * dust_velocity[1], 0),
        ]
    )
    return (rate, terms)


def coupled_gas(gas_velocity, totals):
    return (gas_velocity + totals[1:]) / (1.0 + totals[0])


def assemble(new_density, dust_velocity, gas_next, rate):
    dust_next = (dust_velocity + rate[None] * gas_next[:, None]) / (1.0 + rate[None])
    dust = jnp.concatenate([new_density[None, :-1], dust_next], axis=0)
    gas = jnp.concatenate([new_density[None, -1], gas_next], axis=0)
    return dust, gas


def xor_pairs(count, bit):
    return [(i, i ^ bit) for i in range(count)]


def mirror_pairs(count, block):
    blocks = count // block
    return [(i, (blocks - 1 - i // block) * block + i % block) for i in range(count)]


def global_max(value, axes):
    count = 1
    for axis in axes:
        count *= lax.axis_size(axis)
    spread = jnp.broadcast_to(value, (count,))
    return jnp.max(lax.all_to_all(spread, axes, 0, 0, tiled=True))


def split_rounds(part, axis, rounds):
    index = lax.axis_index(axis)
    done = []
    for bit in rounds:
        dim = 0 if part.shape[0] % 2 == 0 and part.shape[0] >= 16 else 1
        half = part.shape[dim] // 2
        low = lax.slice_in_dim(part, 0, half, axis=dim)
        high = lax.slice_in_dim(part, half, None, axis=dim)
        upper = (index // bit) % 2 == 1
        keep = jnp.where(upper, high, low)
        send = jnp.where(upper, low, high)
        part = keep + lax.ppermute(send, axis, xor_pairs(lax.axis_size(axis), bit))
        done.append((bit, dim))
    return part, done


def join_rounds(part, axis, done):
    index = lax.axis_index(axis)
    for bit, dim in reversed(done):
        other = lax.ppermute(part, axis, xor_pairs(lax.axis_size(axis), bit))
        upper = (index // bit) % 2 == 1
        part = jnp.where(
            upper,
            jnp.concatenate([other, part], axis=dim),
            jnp.concatenate([part, other], axis=dim),
        )
    return part


def species_sum(block, axis, first_done=()):
    count = lax.axis_size(axis)
    index = lax.axis_index(axis)
    low_bits = [bit for bit in (1, 2) if bit < count]
    taken = [bit for bit, dim in first_done]
    part, done = split_rounds(block, axis, [bit for bit in low_bits if bit not in taken])
    done = list(first_done) + done
    block_size = 2 * low_bits[-1] if low_bits else 1
    bit = block_size
    while bit < count:
        pairs = mirror_pairs(count, block_size) if 2 * bit >= count else xor_pairs(count, bit)
        other = lax.ppermute(part, axis, pairs)
        part = part + other
        bit *= 2
    return join_rounds(part, axis, done)


def drag_sums(step_time, stop_times, upper, dust, gas_density, divergence, total_species):
    local_species = dust.shape[1]
    gas_new = gas_density - step_time * divergence[local_species]
    fresh = dust[0] - step_time * divergence[:local_species]
    rate = step_time * gas_new[None] / stop_times[:, None, None]
    weight = fresh / (total_species * gas_new[None]) * rate / (1.0 + rate)
    totals = jnp.concatenate(
        [jnp.sum(weight, 0), jnp.sum(weight * dust[1], 0), jnp.sum(weight * dust[2], 0)], axis=0
    )
    half = totals.shape[0] // 2
    low, high = totals[:half], totals[half:]
    keep = jnp.where(upper, high, low)
    send = jnp.where(upper, low, high)
    density = jnp.concatenate([fresh, gas_new[None]], axis=0)
    return density, rate, keep, send


def advance(wide, margin, tile_rows, stop_times, total_species):
    interior = lax.slice_in_dim(wide, margin, margin + tile_rows, axis=2)
    local_top = jnp.max(jnp.abs(interior[1]) + jnp.abs(interior[2]))
    fastest = global_max(local_top, ("space", "species"))
    step_time = courant / (sound_speed + fastest)
    density = wide[0]
    radial = wide[1]
    azimuth = wide[2]
    div_azimuth = face_divergence(density, azimuth, 1)
    inner_density = density[:, 2:-2]
    inner_radial = radial[:, 2:-2]
    zero_pad = ((0, 0), (0, 0), (2, 2))
    div_radial = face_divergence(
        jnp.pad(inner_density, zero_pad), jnp.pad(inner_radial, zero_pad), 2
    )
    divergence = div_azimuth + div_radial
    dust = interior[:, :-1]
    upper = lax.axis_index("species") % 2 == 1
    new_density, rate, keep, send = drag_sums(
        step_time, stop_times, upper, dust, inner_density[-1], divergence, total_species
    )
    gas_density = density[-1]
    inner_gas = gas_density[2:-2]
    grad_azimuth = 0.5 * (gas_density[3:-1] - gas_density[1:-3])
    edge_gas = jnp.pad(inner_gas, ((0, 0), (1, 1)), mode="edge")
    grad_radial = 0.5 * (edge_gas[:, 2:] - edge_gas[:, :-2])
    push = step_time * sound_sq / inner_gas
    gas_velocity = jnp.stack(
        [inner_radial[-1] - push * grad_radial, azimuth[-1, 2:-2] - push * grad_azimuth]
    )
    dust_velocity = jnp.stack([inner_radial[:-1], azimuth[:-1, 2:-2]])
    part = keep + lax.ppermute(send, "species", xor_pairs(lax.axis_size("species"), 1))
    totals = species_sum(part, "species", first_done=[(1, 0)])
    totals = totals.reshape(3, tile_rows, -1)
    gas_next = coupled_gas(gas_velocity, totals)
    return assemble(new_density, dust_velocity, gas_next, rate)


def local(dust_state, gas_state, species_bin):
    local_species = dust_state.shape[1]
    total_species = local_species * lax.axis_size("species")
    tile_rows = dust_state.shape[2]
    fluid = jnp.concatenate([dust_state, gas_state[:, None]], axis=1)
    stop_times = stop_floor * jnp.exp(
        stop_span * species_bin.astype(jnp.float32) / (total_species - 1)
    )
    for iteration in range(STEPS):
        wide = padded(fluid, (("space", 2),), 2)
        dust, gas = advance(wide, 2, tile_rows, stop_times, total_species)
        fluid = jnp.concatenate([dust, gas[:, None]], axis=1)
    return (dust, gas)


def solution(mesh):
    placed = (P(None, "species", "space", None), P(None, "space", None), P("species"))
    return jax.shard_map(
        local,
        mesh=mesh,
        in_specs=placed,
        out_specs=(P(None, "species", "space", None), P(None, "space", None)),
        check_vma=False,
    )
```

```python
import jax
import jax.numpy as jnp
from jax import lax
from jax.sharding import PartitionSpec as P

STEPS = 2


courant = 0.25
sound_speed = 1.0
sound_sq = 1.0
stop_floor = 0.003
stop_span = 6.907755


def padded(block, sides, width):
    for axis, dim in sides:
        count = lax.axis_size(axis)
        forward = [(i, i + 1) for i in range(count - 1)]
        forward.append((count - 1, 0))
        backward = [(target, source) for source, target in forward]
        low = lax.ppermute(
            lax.slice_in_dim(block, block.shape[dim] - width, None, axis=dim), axis, forward
        )
        high = lax.ppermute(lax.slice_in_dim(block, 0, width, axis=dim), axis, backward)
        block = jnp.concatenate([low, block, high], axis=dim)
    return block


def window(values, start, length, along):
    return lax.slice_in_dim(values, start, start + length, axis=along)


def face_divergence(density, velocity, along):
    faces = density.shape[along] - 3
    back_two = window(density, 0, faces, along)
    here = window(density, 1, faces, along)
    ahead = window(density, 2, faces, along)
    ahead_two = window(density, 3, faces, along)
    face_speed = 0.5 * (window(velocity, 1, faces, along) + window(velocity, 2, faces, along))
    flux = jnp.maximum(face_speed, 0.0) * (1.5 * here - 0.5 * back_two) + jnp.minimum(
        face_speed, 0.0
    ) * (1.5 * ahead - 0.5 * ahead_two)
    return window(flux, 1, faces - 1, along) - window(flux, 0, faces - 1, along)


def moved(fluid, step_time):
    density = fluid[0]
    radial = fluid[1]
    azimuth = fluid[2]
    div_azimuth = face_divergence(density, azimuth, 1)
    inner_density = density[:, 2:-2]
    inner_radial = radial[:, 2:-2]
    zero_pad = ((0, 0), (0, 0), (2, 2))
    div_radial = face_divergence(
        jnp.pad(inner_density, zero_pad), jnp.pad(inner_radial, zero_pad), 2
    )
    new_density = inner_density - step_time * (div_azimuth + div_radial)
    gas_density = density[-1]
    inner_gas = gas_density[2:-2]
    grad_azimuth = 0.5 * (gas_density[3:-1] - gas_density[1:-3])
    edge_gas = jnp.pad(inner_gas, ((0, 0), (1, 1)), mode="edge")
    grad_radial = 0.5 * (edge_gas[:, 2:] - edge_gas[:, :-2])
    push = step_time * sound_sq / inner_gas
    gas_velocity = jnp.stack(
        [inner_radial[-1] - push * grad_radial, azimuth[-1, 2:-2] - push * grad_azimuth]
    )
    dust_velocity = jnp.stack([inner_radial[:-1], azimuth[:-1, 2:-2]])
    return (new_density, gas_velocity, dust_velocity)


def drag_terms(new_density, dust_velocity, stop_times, step_time, total_species):
    gas_new = new_density[-1]
    rate = step_time * gas_new[None] / stop_times[:, None, None]
    weight = new_density[:-1] / (total_species * gas_new[None]) * rate / (1.0 + rate)
    terms = jnp.stack(
        [
            jnp.sum(weight, 0),
            jnp.sum(weight * dust_velocity[0], 0),
            jnp.sum(weight * dust_velocity[1], 0),
        ]
    )
    return (rate, terms)


def coupled_gas(gas_velocity, totals):
    return (gas_velocity + totals[1:]) / (1.0 + totals[0])


def assemble(new_density, dust_velocity, gas_next, rate):
    dust_next = (dust_velocity + rate[None] * gas_next[:, None]) / (1.0 + rate[None])
    dust = jnp.concatenate([new_density[None, :-1], dust_next], axis=0)
    gas = jnp.concatenate([new_density[None, -1], gas_next], axis=0)
    return dust, gas


def xor_pairs(count, bit):
    return [(i, i ^ bit) for i in range(count)]


def mirror_pairs(count, block):
    blocks = count // block
    return [(i, (blocks - 1 - i // block) * block + i % block) for i in range(count)]


def global_max(value, axes):
    count = 1
    for axis in axes:
        count *= lax.axis_size(axis)
    spread = jnp.broadcast_to(value, (count,))
    return jnp.max(lax.all_to_all(spread, axes, 0, 0, tiled=True))


def split_rounds(part, axis, rounds):
    index = lax.axis_index(axis)
    done = []
    for bit in rounds:
        dim = 0 if part.shape[0] % 2 == 0 and part.shape[0] >= 16 else 1
        half = part.shape[dim] // 2
        low = lax.slice_in_dim(part, 0, half, axis=dim)
        high = lax.slice_in_dim(part, half, None, axis=dim)
        upper = (index // bit) % 2 == 1
        keep = jnp.where(upper, high, low)
        send = jnp.where(upper, low, high)
        part = keep + lax.ppermute(send, axis, xor_pairs(lax.axis_size(axis), bit))
        done.append((bit, dim))
    return part, done


def join_rounds(part, axis, done):
    index = lax.axis_index(axis)
    for bit, dim in reversed(done):
        other = lax.ppermute(part, axis, xor_pairs(lax.axis_size(axis), bit))
        upper = (index // bit) % 2 == 1
        part = jnp.where(
            upper,
            jnp.concatenate([other, part], axis=dim),
            jnp.concatenate([part, other], axis=dim),
        )
    return part


def species_sum(block, axis, first_done=()):
    count = lax.axis_size(axis)
    index = lax.axis_index(axis)
    low_bits = [bit for bit in (1, 2) if bit < count]
    taken = [bit for bit, dim in first_done]
    part, done = split_rounds(block, axis, [bit for bit in low_bits if bit not in taken])
    done = list(first_done) + done
    block_size = 2 * low_bits[-1] if low_bits else 1
    bit = block_size
    while bit < count:
        pairs = mirror_pairs(count, block_size) if 2 * bit >= count else xor_pairs(count, bit)
        other = lax.ppermute(part, axis, pairs)
        upper = (index // bit) % 2 == 1 if 2 * bit < count else index >= count // 2
        part = jnp.where(upper, other + part, part + other)
        bit *= 2
    return join_rounds(part, axis, done)


def drag_sums(step_time, stop_times, upper, dust, gas_density, divergence, total_species):
    local_species = dust.shape[1]
    gas_new = gas_density - step_time * divergence[local_species]
    fresh = dust[0] - step_time * divergence[:local_species]
    rate = step_time * gas_new[None] / stop_times[:, None, None]
    weight = fresh / (total_species * gas_new[None]) * rate / (1.0 + rate)
    totals = jnp.concatenate(
        [jnp.sum(weight, 0), jnp.sum(weight * dust[1], 0), jnp.sum(weight * dust[2], 0)], axis=0
    )
    half = totals.shape[0] // 2
    low, high = totals[:half], totals[half:]
    keep = jnp.where(upper, high, low)
    send = jnp.where(upper, low, high)
    density = jnp.concatenate([fresh, gas_new[None]], axis=0)
    return density, rate, keep, send


def advance(wide, margin, tile_rows, stop_times, total_species, local_top=None):
    interior = lax.slice_in_dim(wide, margin, margin + tile_rows, axis=2)
    if local_top is None:
        local_top = jnp.max(jnp.abs(interior[1]) + jnp.abs(interior[2]))
    fastest = global_max(local_top, ("space", "species"))
    step_time = courant / (sound_speed + fastest)
    density = wide[0]
    radial = wide[1]
    azimuth = wide[2]
    div_azimuth = face_divergence(density, azimuth, 1)
    inner_density = density[:, 2:-2]
    inner_radial = radial[:, 2:-2]
    zero_pad = ((0, 0), (0, 0), (2, 2))
    div_radial = face_divergence(
        jnp.pad(inner_density, zero_pad), jnp.pad(inner_radial, zero_pad), 2
    )
    divergence = div_azimuth + div_radial
    dust = interior[:, :-1]
    upper = lax.axis_index("species") % 2 == 1
    new_density, rate, keep, send = drag_sums(
        step_time, stop_times, upper, dust, inner_density[-1], divergence, total_species
    )
    gas_density = density[-1]
    inner_gas = gas_density[2:-2]
    grad_azimuth = 0.5 * (gas_density[3:-1] - gas_density[1:-3])
    edge_gas = jnp.pad(inner_gas, ((0, 0), (1, 1)), mode="edge")
    grad_radial = 0.5 * (edge_gas[:, 2:] - edge_gas[:, :-2])
    push = step_time * sound_sq / inner_gas
    gas_velocity = jnp.stack(
        [inner_radial[-1] - push * grad_radial, azimuth[-1, 2:-2] - push * grad_azimuth]
    )
    dust_velocity = jnp.stack([inner_radial[:-1], azimuth[:-1, 2:-2]])
    part = keep + lax.ppermute(send, "species", xor_pairs(lax.axis_size("species"), 1))
    totals = species_sum(part, "species", first_done=[(1, 0)])
    totals = totals.reshape(3, tile_rows, -1)
    gas_next = coupled_gas(gas_velocity, totals)
    return assemble(new_density, dust_velocity, gas_next, rate)


def local(dust_state, gas_state, species_bin):
    local_species = dust_state.shape[1]
    total_species = local_species * lax.axis_size("species")
    tile_rows = dust_state.shape[2]
    fluid = jnp.concatenate([dust_state, gas_state[:, None]], axis=1)
    stop_times = stop_floor * jnp.exp(
        stop_span * species_bin.astype(jnp.float32) / (total_species - 1)
    )
    for iteration in range(STEPS):
        wide = padded(fluid, (("space", 2),), 2)
        local_top = None
        if iteration == 0:
            interior = lax.slice_in_dim(wide, 2, 2 + tile_rows, axis=2)
            local_top = jnp.max(jnp.abs(interior[1]) + jnp.abs(interior[2]))
            landed = wide[0, 0, 0, 0] + wide[0, 0, -1, 0]
            local_top = jnp.maximum(local_top, 0.0 * landed)
        dust, gas = advance(wide, 2, tile_rows, stop_times, total_species, local_top)
        fluid = jnp.concatenate([dust, gas[:, None]], axis=1)
    return (dust, gas)


def solution(mesh):
    placed = (P(None, "species", "space", None), P(None, "space", None), P("species"))
    return jax.shard_map(
        local,
        mesh=mesh,
        in_specs=placed,
        out_specs=(P(None, "species", "space", None), P(None, "space", None)),
        check_vma=False,
    )
```

```python
import jax
import jax.numpy as jnp
from jax import lax
from jax.sharding import PartitionSpec as P

STEPS = 2


courant = 0.25
sound_speed = 1.0
sound_sq = 1.0
stop_floor = 0.003
stop_span = 6.907755


def padded(block, sides, width):
    for axis, dim in sides:
        count = lax.axis_size(axis)
        forward = [(i, i + 1) for i in range(count - 1)]
        forward.append((count - 1, 0))
        backward = [(target, source) for source, target in forward]
        low = lax.ppermute(
            lax.slice_in_dim(block, block.shape[dim] - width, None, axis=dim), axis, forward
        )
        high = lax.ppermute(lax.slice_in_dim(block, 0, width, axis=dim), axis, backward)
        block = jnp.concatenate([low, block, high], axis=dim)
    return block


def window(values, start, length, along):
    return lax.slice_in_dim(values, start, start + length, axis=along)


def face_divergence(density, velocity, along):
    faces = density.shape[along] - 3
    back_two = window(density, 0, faces, along)
    here = window(density, 1, faces, along)
    ahead = window(density, 2, faces, along)
    ahead_two = window(density, 3, faces, along)
    face_speed = 0.5 * (window(velocity, 1, faces, along) + window(velocity, 2, faces, along))
    flux = jnp.maximum(face_speed, 0.0) * (1.5 * here - 0.5 * back_two) + jnp.minimum(
        face_speed, 0.0
    ) * (1.5 * ahead - 0.5 * ahead_two)
    return window(flux, 1, faces - 1, along) - window(flux, 0, faces - 1, along)


def moved(fluid, step_time):
    density = fluid[0]
    radial = fluid[1]
    azimuth = fluid[2]
    div_azimuth = face_divergence(density, azimuth, 1)
    inner_density = density[:, 2:-2]
    inner_radial = radial[:, 2:-2]
    zero_pad = ((0, 0), (0, 0), (2, 2))
    div_radial = face_divergence(
        jnp.pad(inner_density, zero_pad), jnp.pad(inner_radial, zero_pad), 2
    )
    new_density = inner_density - step_time * (div_azimuth + div_radial)
    gas_density = density[-1]
    inner_gas = gas_density[2:-2]
    grad_azimuth = 0.5 * (gas_density[3:-1] - gas_density[1:-3])
    edge_gas = jnp.pad(inner_gas, ((0, 0), (1, 1)), mode="edge")
    grad_radial = 0.5 * (edge_gas[:, 2:] - edge_gas[:, :-2])
    push = step_time * sound_sq / inner_gas
    gas_velocity = jnp.stack(
        [inner_radial[-1] - push * grad_radial, azimuth[-1, 2:-2] - push * grad_azimuth]
    )
    dust_velocity = jnp.stack([inner_radial[:-1], azimuth[:-1, 2:-2]])
    return (new_density, gas_velocity, dust_velocity)


def drag_terms(new_density, dust_velocity, stop_times, step_time, total_species):
    gas_new = new_density[-1]
    rate = step_time * gas_new[None] / stop_times[:, None, None]
    weight = new_density[:-1] / (total_species * gas_new[None]) * rate / (1.0 + rate)
    terms = jnp.stack(
        [
            jnp.sum(weight, 0),
            jnp.sum(weight * dust_velocity[0], 0),
            jnp.sum(weight * dust_velocity[1], 0),
        ]
    )
    return (rate, terms)


def coupled_gas(gas_velocity, totals):
    return (gas_velocity + totals[1:]) / (1.0 + totals[0])


def assemble(new_density, dust_velocity, gas_next, rate):
    dust_next = (dust_velocity + rate[None] * gas_next[:, None]) / (1.0 + rate[None])
    dust = jnp.concatenate([new_density[None, :-1], dust_next], axis=0)
    gas = jnp.concatenate([new_density[None, -1], gas_next], axis=0)
    return dust, gas


def xor_pairs(count, bit):
    return [(i, i ^ bit) for i in range(count)]


def mirror_pairs(count, block):
    blocks = count // block
    return [(i, (blocks - 1 - i // block) * block + i % block) for i in range(count)]


def global_max(value, axes):
    count = 1
    for axis in axes:
        count *= lax.axis_size(axis)
    spread = jnp.broadcast_to(value, (count,))
    return jnp.max(lax.all_to_all(spread, axes, 0, 0, tiled=True))


def split_rounds(part, axis, rounds):
    index = lax.axis_index(axis)
    done = []
    for bit in rounds:
        dim = 0 if part.shape[0] % 2 == 0 and part.shape[0] >= 16 else 1
        half = part.shape[dim] // 2
        low = lax.slice_in_dim(part, 0, half, axis=dim)
        high = lax.slice_in_dim(part, half, None, axis=dim)
        upper = (index // bit) % 2 == 1
        keep = jnp.where(upper, high, low)
        send = jnp.where(upper, low, high)
        part = keep + lax.ppermute(send, axis, xor_pairs(lax.axis_size(axis), bit))
        done.append((bit, dim))
    return part, done


def join_rounds(part, axis, done):
    index = lax.axis_index(axis)
    for bit, dim in reversed(done):
        other = lax.ppermute(part, axis, xor_pairs(lax.axis_size(axis), bit))
        upper = (index // bit) % 2 == 1
        part = jnp.where(
            upper,
            jnp.concatenate([other, part], axis=dim),
            jnp.concatenate([part, other], axis=dim),
        )
    return part


def species_sum(block, axis, first_done=()):
    count = lax.axis_size(axis)
    index = lax.axis_index(axis)
    low_bits = [bit for bit in (1, 2) if bit < count]
    taken = [bit for bit, dim in first_done]
    part, done = split_rounds(block, axis, [bit for bit in low_bits if bit not in taken])
    done = list(first_done) + done
    block_size = 2 * low_bits[-1] if low_bits else 1
    if count // block_size == 8:
        rounds = (
            lambda z: z ^ 1,
            lambda z: (z + 1 if z % 2 == 1 else z - 1) % 8,
            lambda z: (3 - z) % 8 if z % 4 in (0, 3) else 7 - z,
        )
        for partner in rounds:
            pairs = [(i, partner(i // block_size) * block_size + i % block_size) for i in range(count)]
            part = part + lax.ppermute(part, axis, pairs)
        return join_rounds(part, axis, done)
    bit = block_size
    while bit < count:
        pairs = mirror_pairs(count, block_size) if 2 * bit >= count else xor_pairs(count, bit)
        other = lax.ppermute(part, axis, pairs)
        upper = (index // bit) % 2 == 1 if 2 * bit < count else index >= count // 2
        part = jnp.where(upper, other + part, part + other)
        bit *= 2
    return join_rounds(part, axis, done)


def drag_sums(step_time, stop_times, upper, dust, gas_density, divergence, total_species):
    local_species = dust.shape[1]
    gas_new = gas_density - step_time * divergence[local_species]
    fresh = dust[0] - step_time * divergence[:local_species]
    rate = step_time * gas_new[None] / stop_times[:, None, None]
    weight = fresh / (total_species * gas_new[None]) * rate / (1.0 + rate)
    totals = jnp.concatenate(
        [jnp.sum(weight, 0), jnp.sum(weight * dust[1], 0), jnp.sum(weight * dust[2], 0)], axis=0
    )
    half = totals.shape[0] // 2
    low, high = totals[:half], totals[half:]
    keep = jnp.where(upper, high, low)
    send = jnp.where(upper, low, high)
    density = jnp.concatenate([fresh, gas_new[None]], axis=0)
    return density, rate, keep, send


def advance(wide, margin, tile_rows, stop_times, total_species):
    interior = lax.slice_in_dim(wide, margin, margin + tile_rows, axis=2)
    local_top = jnp.max(jnp.abs(interior[1]) + jnp.abs(interior[2]))
    fastest = global_max(local_top, ("space", "species"))
    step_time = courant / (sound_speed + fastest)
    density = wide[0]
    radial = wide[1]
    azimuth = wide[2]
    div_azimuth = face_divergence(density, azimuth, 1)
    inner_density = density[:, 2:-2]
    inner_radial = radial[:, 2:-2]
    zero_pad = ((0, 0), (0, 0), (2, 2))
    div_radial = face_divergence(
        jnp.pad(inner_density, zero_pad), jnp.pad(inner_radial, zero_pad), 2
    )
    divergence = div_azimuth + div_radial
    dust = interior[:, :-1]
    upper = lax.axis_index("species") % 2 == 1
    new_density, rate, keep, send = drag_sums(
        step_time, stop_times, upper, dust, inner_density[-1], divergence, total_species
    )
    gas_density = density[-1]
    inner_gas = gas_density[2:-2]
    grad_azimuth = 0.5 * (gas_density[3:-1] - gas_density[1:-3])
    edge_gas = jnp.pad(inner_gas, ((0, 0), (1, 1)), mode="edge")
    grad_radial = 0.5 * (edge_gas[:, 2:] - edge_gas[:, :-2])
    push = step_time * sound_sq / inner_gas
    gas_velocity = jnp.stack(
        [inner_radial[-1] - push * grad_radial, azimuth[-1, 2:-2] - push * grad_azimuth]
    )
    dust_velocity = jnp.stack([inner_radial[:-1], azimuth[:-1, 2:-2]])
    part = keep + lax.ppermute(send, "species", xor_pairs(lax.axis_size("species"), 1))
    totals = species_sum(part, "species", first_done=[(1, 0)])
    totals = totals.reshape(3, tile_rows, -1)
    gas_next = coupled_gas(gas_velocity, totals)
    return assemble(new_density, dust_velocity, gas_next, rate)


def local(dust_state, gas_state, species_bin):
    local_species = dust_state.shape[1]
    total_species = local_species * lax.axis_size("species")
    tile_rows = dust_state.shape[2]
    fluid = jnp.concatenate([dust_state, gas_state[:, None]], axis=1)
    stop_times = stop_floor * jnp.exp(
        stop_span * species_bin.astype(jnp.float32) / (total_species - 1)
    )
    for iteration in range(STEPS):
        wide = padded(fluid, (("space", 2),), 2)
        dust, gas = advance(wide, 2, tile_rows, stop_times, total_species)
        fluid = jnp.concatenate([dust, gas[:, None]], axis=1)
    return (dust, gas)


def solution(mesh):
    placed = (P(None, "species", "space", None), P(None, "space", None), P("species"))
    return jax.shard_map(
        local,
        mesh=mesh,
        in_specs=placed,
        out_specs=(P(None, "species", "space", None), P(None, "space", None)),
        check_vma=False,
    )
```

```python
import jax
import jax.numpy as jnp
from jax import lax
from jax.sharding import PartitionSpec as P

STEPS = 2


courant = 0.25
sound_speed = 1.0
sound_sq = 1.0
stop_floor = 0.003
stop_span = 6.907755


def padded(block, sides, width):
    for axis, dim in sides:
        count = lax.axis_size(axis)
        forward = [(i, i + 1) for i in range(count - 1)]
        forward.append((count - 1, 0))
        backward = [(target, source) for source, target in forward]
        low = lax.ppermute(
            lax.slice_in_dim(block, block.shape[dim] - width, None, axis=dim), axis, forward
        )
        high = lax.ppermute(lax.slice_in_dim(block, 0, width, axis=dim), axis, backward)
        block = jnp.concatenate([low, block, high], axis=dim)
    return block


def window(values, start, length, along):
    return lax.slice_in_dim(values, start, start + length, axis=along)


def face_divergence(density, velocity, along):
    faces = density.shape[along] - 3
    back_two = window(density, 0, faces, along)
    here = window(density, 1, faces, along)
    ahead = window(density, 2, faces, along)
    ahead_two = window(density, 3, faces, along)
    face_speed = 0.5 * (window(velocity, 1, faces, along) + window(velocity, 2, faces, along))
    flux = jnp.maximum(face_speed, 0.0) * (1.5 * here - 0.5 * back_two) + jnp.minimum(
        face_speed, 0.0
    ) * (1.5 * ahead - 0.5 * ahead_two)
    return window(flux, 1, faces - 1, along) - window(flux, 0, faces - 1, along)


def moved(fluid, step_time):
    density = fluid[0]
    radial = fluid[1]
    azimuth = fluid[2]
    div_azimuth = face_divergence(density, azimuth, 1)
    inner_density = density[:, 2:-2]
    inner_radial = radial[:, 2:-2]
    zero_pad = ((0, 0), (0, 0), (2, 2))
    div_radial = face_divergence(
        jnp.pad(inner_density, zero_pad), jnp.pad(inner_radial, zero_pad), 2
    )
    new_density = inner_density - step_time * (div_azimuth + div_radial)
    gas_density = density[-1]
    inner_gas = gas_density[2:-2]
    grad_azimuth = 0.5 * (gas_density[3:-1] - gas_density[1:-3])
    edge_gas = jnp.pad(inner_gas, ((0, 0), (1, 1)), mode="edge")
    grad_radial = 0.5 * (edge_gas[:, 2:] - edge_gas[:, :-2])
    push = step_time * sound_sq / inner_gas
    gas_velocity = jnp.stack(
        [inner_radial[-1] - push * grad_radial, azimuth[-1, 2:-2] - push * grad_azimuth]
    )
    dust_velocity = jnp.stack([inner_radial[:-1], azimuth[:-1, 2:-2]])
    return (new_density, gas_velocity, dust_velocity)


def drag_terms(new_density, dust_velocity, stop_times, step_time, total_species):
    gas_new = new_density[-1]
    rate = step_time * gas_new[None] / stop_times[:, None, None]
    weight = new_density[:-1] / (total_species * gas_new[None]) * rate / (1.0 + rate)
    terms = jnp.stack(
        [
            jnp.sum(weight, 0),
            jnp.sum(weight * dust_velocity[0], 0),
            jnp.sum(weight * dust_velocity[1], 0),
        ]
    )
    return (rate, terms)


def coupled_gas(gas_velocity, totals):
    return (gas_velocity + totals[1:]) / (1.0 + totals[0])


def assemble(new_density, dust_velocity, gas_next, rate):
    dust_next = (dust_velocity + rate[None] * gas_next[:, None]) / (1.0 + rate[None])
    dust = jnp.concatenate([new_density[None, :-1], dust_next], axis=0)
    gas = jnp.concatenate([new_density[None, -1], gas_next], axis=0)
    return dust, gas


def xor_pairs(count, bit):
    return [(i, i ^ bit) for i in range(count)]


def mirror_pairs(count, block):
    blocks = count // block
    return [(i, (blocks - 1 - i // block) * block + i % block) for i in range(count)]


def global_max(value, axes):
    count = 1
    for axis in axes:
        count *= lax.axis_size(axis)
    spread = jnp.broadcast_to(value, (count,))
    return jnp.max(lax.all_to_all(spread, axes, 0, 0, tiled=True))


def split_rounds(part, axis, rounds):
    index = lax.axis_index(axis)
    done = []
    for bit in rounds:
        dim = 0 if part.shape[0] % 2 == 0 and part.shape[0] >= 16 else 1
        half = part.shape[dim] // 2
        low = lax.slice_in_dim(part, 0, half, axis=dim)
        high = lax.slice_in_dim(part, half, None, axis=dim)
        upper = (index // bit) % 2 == 1
        keep = jnp.where(upper, high, low)
        send = jnp.where(upper, low, high)
        part = keep + lax.ppermute(send, axis, xor_pairs(lax.axis_size(axis), bit))
        done.append((bit, dim))
    return part, done


def join_rounds(part, axis, done):
    index = lax.axis_index(axis)
    for bit, dim in reversed(done):
        other = lax.ppermute(part, axis, xor_pairs(lax.axis_size(axis), bit))
        upper = (index // bit) % 2 == 1
        part = jnp.where(
            upper,
            jnp.concatenate([other, part], axis=dim),
            jnp.concatenate([part, other], axis=dim),
        )
    return part


def species_sum(block, axis, first_done=(), finish=None):
    count = lax.axis_size(axis)
    index = lax.axis_index(axis)
    low_bits = [bit for bit in (1, 2) if bit < count]
    taken = [bit for bit, dim in first_done]
    part, done = split_rounds(block, axis, [bit for bit in low_bits if bit not in taken])
    done = list(first_done) + done
    block_size = 2 * low_bits[-1] if low_bits else 1
    if count // block_size == 8:
        rounds = (
            lambda z: z ^ 1,
            lambda z: (z + 1 if z % 2 == 1 else z - 1) % 8,
            lambda z: (3 - z) % 8 if z % 4 in (0, 3) else 7 - z,
        )
        for partner in rounds:
            pairs = [(i, partner(i // block_size) * block_size + i % block_size) for i in range(count)]
            part = part + lax.ppermute(part, axis, pairs)
        if finish is not None:
            part = finish(part)
        return join_rounds(part, axis, done)
    bit = block_size
    while bit < count:
        pairs = mirror_pairs(count, block_size) if 2 * bit >= count else xor_pairs(count, bit)
        other = lax.ppermute(part, axis, pairs)
        upper = (index // bit) % 2 == 1 if 2 * bit < count else index >= count // 2
        part = jnp.where(upper, other + part, part + other)
        bit *= 2
    if finish is not None:
        part = finish(part)
    return join_rounds(part, axis, done)


def drag_sums(step_time, stop_times, upper, dust, gas_density, divergence, total_species):
    local_species = dust.shape[1]
    gas_new = gas_density - step_time * divergence[local_species]
    fresh = dust[0] - step_time * divergence[:local_species]
    rate = step_time * gas_new[None] / stop_times[:, None, None]
    weight = fresh / (total_species * gas_new[None]) * rate / (1.0 + rate)
    sums = jnp.stack([jnp.sum(weight, 0), jnp.sum(weight * dust[1], 0), jnp.sum(weight * dust[2], 0)])
    rows, lanes = sums.shape[1:]
    totals = sums.reshape(3, 4, rows // 4, lanes).transpose(1, 0, 2, 3).reshape(-1, lanes)
    half = totals.shape[0] // 2
    low, high = totals[:half], totals[half:]
    keep = jnp.where(upper, high, low)
    send = jnp.where(upper, low, high)
    density = jnp.concatenate([fresh, gas_new[None]], axis=0)
    return density, rate, keep, send


def advance(wide, margin, tile_rows, stop_times, total_species):
    interior = lax.slice_in_dim(wide, margin, margin + tile_rows, axis=2)
    local_top = jnp.max(jnp.abs(interior[1]) + jnp.abs(interior[2]))
    fastest = global_max(local_top, ("space", "species"))
    step_time = courant / (sound_speed + fastest)
    density = wide[0]
    radial = wide[1]
    azimuth = wide[2]
    div_azimuth = face_divergence(density, azimuth, 1)
    inner_density = density[:, 2:-2]
    inner_radial = radial[:, 2:-2]
    zero_pad = ((0, 0), (0, 0), (2, 2))
    div_radial = face_divergence(
        jnp.pad(inner_density, zero_pad), jnp.pad(inner_radial, zero_pad), 2
    )
    divergence = div_azimuth + div_radial
    dust = interior[:, :-1]
    upper = lax.axis_index("species") % 2 == 1
    new_density, rate, keep, send = drag_sums(
        step_time, stop_times, upper, dust, inner_density[-1], divergence, total_species
    )
    gas_density = density[-1]
    inner_gas = gas_density[2:-2]
    grad_azimuth = 0.5 * (gas_density[3:-1] - gas_density[1:-3])
    edge_gas = jnp.pad(inner_gas, ((0, 0), (1, 1)), mode="edge")
    grad_radial = 0.5 * (edge_gas[:, 2:] - edge_gas[:, :-2])
    push = step_time * sound_sq / inner_gas
    gas_velocity = jnp.stack(
        [inner_radial[-1] - push * grad_radial, azimuth[-1, 2:-2] - push * grad_azimuth]
    )
    dust_velocity = jnp.stack([inner_radial[:-1], azimuth[:-1, 2:-2]])
    part = keep + lax.ppermute(send, "species", xor_pairs(lax.axis_size("species"), 1))
    species = lax.axis_index("species")
    quarter = 2 * (species % 2) + (species // 2) % 2
    rows = tile_rows // 4

    def finish(block):
        own = block.reshape(3, rows, -1)
        star = lax.dynamic_slice_in_dim(gas_velocity, quarter * rows, rows, axis=1)
        return coupled_gas(star, own).reshape(2 * rows, -1)

    joined = species_sum(part, "species", first_done=[(1, 0)], finish=finish)
    gas_next = joined.reshape(4, 2, rows, -1).transpose(1, 0, 2, 3).reshape(2, tile_rows, -1)
    return assemble(new_density, dust_velocity, gas_next, rate)


def local(dust_state, gas_state, species_bin):
    local_species = dust_state.shape[1]
    total_species = local_species * lax.axis_size("species")
    tile_rows = dust_state.shape[2]
    fluid = jnp.concatenate([dust_state, gas_state[:, None]], axis=1)
    stop_times = stop_floor * jnp.exp(
        stop_span * species_bin.astype(jnp.float32) / (total_species - 1)
    )
    for iteration in range(STEPS):
        wide = padded(fluid, (("space", 2),), 2)
        dust, gas = advance(wide, 2, tile_rows, stop_times, total_species)
        fluid = jnp.concatenate([dust, gas[:, None]], axis=1)
    return (dust, gas)


def solution(mesh):
    placed = (P(None, "species", "space", None), P(None, "space", None), P("species"))
    return jax.shard_map(
        local,
        mesh=mesh,
        in_specs=placed,
        out_specs=(P(None, "species", "space", None), P(None, "space", None)),
        check_vma=False,
    )
```

```python
import jax
import jax.numpy as jnp
from jax import lax
from jax.sharding import PartitionSpec as P

STEPS = 2


courant = 0.25
sound_speed = 1.0
sound_sq = 1.0
stop_floor = 0.003
stop_span = 6.907755


def padded(block, sides, width):
    for axis, dim in sides:
        count = lax.axis_size(axis)
        forward = [(i, i + 1) for i in range(count - 1)]
        forward.append((count - 1, 0))
        backward = [(target, source) for source, target in forward]
        low = lax.ppermute(
            lax.slice_in_dim(block, block.shape[dim] - width, None, axis=dim), axis, forward
        )
        high = lax.ppermute(lax.slice_in_dim(block, 0, width, axis=dim), axis, backward)
        block = jnp.concatenate([low, block, high], axis=dim)
    return block


def window(values, start, length, along):
    return lax.slice_in_dim(values, start, start + length, axis=along)


def face_divergence(density, velocity, along):
    faces = density.shape[along] - 3
    back_two = window(density, 0, faces, along)
    here = window(density, 1, faces, along)
    ahead = window(density, 2, faces, along)
    ahead_two = window(density, 3, faces, along)
    face_speed = 0.5 * (window(velocity, 1, faces, along) + window(velocity, 2, faces, along))
    flux = jnp.maximum(face_speed, 0.0) * (1.5 * here - 0.5 * back_two) + jnp.minimum(
        face_speed, 0.0
    ) * (1.5 * ahead - 0.5 * ahead_two)
    return window(flux, 1, faces - 1, along) - window(flux, 0, faces - 1, along)


def moved(fluid, step_time):
    density = fluid[0]
    radial = fluid[1]
    azimuth = fluid[2]
    div_azimuth = face_divergence(density, azimuth, 1)
    inner_density = density[:, 2:-2]
    inner_radial = radial[:, 2:-2]
    zero_pad = ((0, 0), (0, 0), (2, 2))
    div_radial = face_divergence(
        jnp.pad(inner_density, zero_pad), jnp.pad(inner_radial, zero_pad), 2
    )
    new_density = inner_density - step_time * (div_azimuth + div_radial)
    gas_density = density[-1]
    inner_gas = gas_density[2:-2]
    grad_azimuth = 0.5 * (gas_density[3:-1] - gas_density[1:-3])
    edge_gas = jnp.pad(inner_gas, ((0, 0), (1, 1)), mode="edge")
    grad_radial = 0.5 * (edge_gas[:, 2:] - edge_gas[:, :-2])
    push = step_time * sound_sq / inner_gas
    gas_velocity = jnp.stack(
        [inner_radial[-1] - push * grad_radial, azimuth[-1, 2:-2] - push * grad_azimuth]
    )
    dust_velocity = jnp.stack([inner_radial[:-1], azimuth[:-1, 2:-2]])
    return (new_density, gas_velocity, dust_velocity)


def drag_terms(new_density, dust_velocity, stop_times, step_time, total_species):
    gas_new = new_density[-1]
    rate = step_time * gas_new[None] / stop_times[:, None, None]
    weight = new_density[:-1] / (total_species * gas_new[None]) * rate / (1.0 + rate)
    terms = jnp.stack(
        [
            jnp.sum(weight, 0),
            jnp.sum(weight * dust_velocity[0], 0),
            jnp.sum(weight * dust_velocity[1], 0),
        ]
    )
    return (rate, terms)


def coupled_gas(gas_velocity, totals):
    return (gas_velocity + totals[1:]) / (1.0 + totals[0])


def assemble(new_density, dust_velocity, gas_next, rate):
    dust_next = (dust_velocity + rate[None] * gas_next[:, None]) / (1.0 + rate[None])
    dust = jnp.concatenate([new_density[None, :-1], dust_next], axis=0)
    gas = jnp.concatenate([new_density[None, -1], gas_next], axis=0)
    return dust, gas


def xor_pairs(count, bit):
    return [(i, i ^ bit) for i in range(count)]


def mirror_pairs(count, block):
    blocks = count // block
    return [(i, (blocks - 1 - i // block) * block + i % block) for i in range(count)]


def global_max(value, axes):
    count = 1
    for axis in axes:
        count *= lax.axis_size(axis)
    spread = jnp.broadcast_to(value, (count,))
    return jnp.max(lax.all_to_all(spread, axes, 0, 0, tiled=True))


def split_rounds(part, axis, rounds):
    index = lax.axis_index(axis)
    done = []
    for bit in rounds:
        dim = 0 if part.shape[0] % 2 == 0 and part.shape[0] >= 16 else 1
        half = part.shape[dim] // 2
        low = lax.slice_in_dim(part, 0, half, axis=dim)
        high = lax.slice_in_dim(part, half, None, axis=dim)
        upper = (index // bit) % 2 == 1
        keep = jnp.where(upper, high, low)
        send = jnp.where(upper, low, high)
        part = keep + lax.ppermute(send, axis, xor_pairs(lax.axis_size(axis), bit))
        done.append((bit, dim))
    return part, done


def join_rounds(part, axis, done):
    index = lax.axis_index(axis)
    for bit, dim in reversed(done):
        other = lax.ppermute(part, axis, xor_pairs(lax.axis_size(axis), bit))
        upper = (index // bit) % 2 == 1
        part = jnp.where(
            upper,
            jnp.concatenate([other, part], axis=dim),
            jnp.concatenate([part, other], axis=dim),
        )
    return part


def species_sum(block, axis, first_done=()):
    count = lax.axis_size(axis)
    index = lax.axis_index(axis)
    low_bits = [bit for bit in (1, 2) if bit < count]
    taken = [bit for bit, dim in first_done]
    part, done = split_rounds(block, axis, [bit for bit in low_bits if bit not in taken])
    done = list(first_done) + done
    block_size = 2 * low_bits[-1] if low_bits else 1
    if count // block_size == 8:
        near = lambda z: z ^ 1
        shifted = lambda z: (z + 1 if z % 2 == 1 else z - 1) % 8
        rounds = (
            (near, shifted, lambda z: (3 - z) % 8 if z % 4 in (0, 3) else 7 - z),
            (shifted, near, lambda z: (5 - z) % 8 if z % 4 in (0, 1) else (9 - z) % 8),
        )
        for step in range(3):
            pairs = [
                (i, rounds[i % 2][step](i // block_size) * block_size + i % block_size)
                for i in range(count)
            ]
            part = part + lax.ppermute(part, axis, pairs)
        return join_rounds(part, axis, done)
    bit = block_size
    while bit < count:
        pairs = mirror_pairs(count, block_size) if 2 * bit >= count else xor_pairs(count, bit)
        other = lax.ppermute(part, axis, pairs)
        upper = (index // bit) % 2 == 1 if 2 * bit < count else index >= count // 2
        part = jnp.where(upper, other + part, part + other)
        bit *= 2
    return join_rounds(part, axis, done)


def drag_sums(step_time, stop_times, upper, dust, gas_density, divergence, total_species):
    local_species = dust.shape[1]
    gas_new = gas_density - step_time * divergence[local_species]
    fresh = dust[0] - step_time * divergence[:local_species]
    rate = step_time * gas_new[None] / stop_times[:, None, None]
    weight = fresh / (total_species * gas_new[None]) * rate / (1.0 + rate)
    totals = jnp.concatenate(
        [jnp.sum(weight, 0), jnp.sum(weight * dust[1], 0), jnp.sum(weight * dust[2], 0)], axis=0
    )
    half = totals.shape[0] // 2
    low, high = totals[:half], totals[half:]
    keep = jnp.where(upper, high, low)
    send = jnp.where(upper, low, high)
    density = jnp.concatenate([fresh, gas_new[None]], axis=0)
    return density, rate, keep, send


def advance(wide, margin, tile_rows, stop_times, total_species):
    interior = lax.slice_in_dim(wide, margin, margin + tile_rows, axis=2)
    local_top = jnp.max(jnp.abs(interior[1]) + jnp.abs(interior[2]))
    fastest = global_max(local_top, ("space", "species"))
    step_time = courant / (sound_speed + fastest)
    density = wide[0]
    radial = wide[1]
    azimuth = wide[2]
    div_azimuth = face_divergence(density, azimuth, 1)
    inner_density = density[:, 2:-2]
    inner_radial = radial[:, 2:-2]
    zero_pad = ((0, 0), (0, 0), (2, 2))
    div_radial = face_divergence(
        jnp.pad(inner_density, zero_pad), jnp.pad(inner_radial, zero_pad), 2
    )
    divergence = div_azimuth + div_radial
    dust = interior[:, :-1]
    upper = lax.axis_index("species") % 2 == 1
    new_density, rate, keep, send = drag_sums(
        step_time, stop_times, upper, dust, inner_density[-1], divergence, total_species
    )
    gas_density = density[-1]
    inner_gas = gas_density[2:-2]
    grad_azimuth = 0.5 * (gas_density[3:-1] - gas_density[1:-3])
    edge_gas = jnp.pad(inner_gas, ((0, 0), (1, 1)), mode="edge")
    grad_radial = 0.5 * (edge_gas[:, 2:] - edge_gas[:, :-2])
    push = step_time * sound_sq / inner_gas
    gas_velocity = jnp.stack(
        [inner_radial[-1] - push * grad_radial, azimuth[-1, 2:-2] - push * grad_azimuth]
    )
    dust_velocity = jnp.stack([inner_radial[:-1], azimuth[:-1, 2:-2]])
    part = keep + lax.ppermute(send, "species", xor_pairs(lax.axis_size("species"), 1))
    totals = species_sum(part, "species", first_done=[(1, 0)])
    totals = totals.reshape(3, tile_rows, -1)
    gas_next = coupled_gas(gas_velocity, totals)
    return assemble(new_density, dust_velocity, gas_next, rate)


def local(dust_state, gas_state, species_bin):
    local_species = dust_state.shape[1]
    total_species = local_species * lax.axis_size("species")
    tile_rows = dust_state.shape[2]
    fluid = jnp.concatenate([dust_state, gas_state[:, None]], axis=1)
    stop_times = stop_floor * jnp.exp(
        stop_span * species_bin.astype(jnp.float32) / (total_species - 1)
    )
    for iteration in range(STEPS):
        wide = padded(fluid, (("space", 2),), 2)
        dust, gas = advance(wide, 2, tile_rows, stop_times, total_species)
        fluid = jnp.concatenate([dust, gas[:, None]], axis=1)
    return (dust, gas)


def solution(mesh):
    placed = (P(None, "species", "space", None), P(None, "space", None), P("species"))
    return jax.shard_map(
        local,
        mesh=mesh,
        in_specs=placed,
        out_specs=(P(None, "species", "space", None), P(None, "space", None)),
        check_vma=False,
    )
```
